256 devices in a mesh: req: 64 (over x, z, core), mlp: 4 (over y).
Axes of the slice: x: 4, y: 4, z: 8, core: 2. Of those that a mesh axis runs over, the one named last changes fastest.
Arguments:
- drafts: bfloat16 [512, 16, 2048], P('req', None, 'mlp'), may hold values from -60 to 60
- slot_of: int32 [512], replicated, may hold values from 0 to 511, as said below
- lengths: int32 [512], P('req'), may hold values from 2 to 256, as said below
- parents: int32 [512, 16], P('req'), may hold values from 0 to 14, as said below
- accepted_tokens: int32 [512, 8], P('req'), may hold values from 0 to 15, as said below
- cached_key_value: bfloat16 [512, 256, 4, 128], P('req', None, 'mlp'), may hold values from -2000 to 2000
- attn_gain: float32 [2048], replicated, may hold values from 0.1 to 1.9
- query_weight: bfloat16 [2048, 768], P(None, 'mlp'), may hold values from -0.125 to 0.125
- key_value_weight: bfloat16 [2048, 512], P(None, 'mlp'), may hold values from -0.125 to 0.125
- w_out: bfloat16 [768, 2048], P('mlp'), may hold values from -0.21875 to 0.21875
- mlp_gain: float32 [2048], replicated, may hold values from 0.1 to 1.9
- w_gate: bfloat16 [2048, 2560], P(None, 'mlp'), may hold values from -0.125 to 0.125
- w_up: bfloat16 [2048, 2560], P(None, 'mlp'), may hold values from -0.125 to 0.125
- w_down: bfloat16 [2560, 2048], P('mlp'), may hold values from -0.125 to 0.125
Outputs:
- layer_output: bfloat16 [512, 16, 2048], P('req', None, 'mlp')
- accepted_kv: bfloat16 [512, 8, 4, 128], P('req', None, 'mlp')
The draws below stay inside these ranges and needn't reach their ends.
Inputs may be any that keep to these rules, and one draw needn't show every extreme that they name: `slot_of`: A permutation of the 512 slots; the cache of slot s is held by index s // 8 of req. Of the 8 requests that arrive on one index of req, at most 1 have their caches on any one index, and that many do for some. `lengths`: some slot holds exactly 256 cached positions. parents[s, 0] = 0 and parents[s, j] < j for j >= 1. accepted_tokens[s, 0] = 0, the entries rise, and each entry is the parent of the next.
All inputs are finite; a program needn't handle non-finite values.
Results may differ from the reference program's by a relative error of at most 0.0095.
Values may be sent and summed in bfloat16 or wider, within the bound.
No kernel may reach another device: no remote copies, remote signals or barrier semaphores. Data moves between devices by JAX's collectives and lax.ppermute only.
A program may use at most 64 MiB of HBM per device.

```python
import math
import jax
import jax.numpy as jnp
from jax import lax

MODEL_DIM = 2048
QUERY_HEADS = 12
KEY_VALUE_HEADS = 4
HEAD_DIM = 64
FFW = 2560
TREE_TOKENS = 16
ACCEPT_LENGTH = 8
CACHE_LIMIT = 256
REQUESTS_PER_KEY = 8
REQUEST_TOTAL = 512
N_REQ = 64
N_MLP = 4


def draw_slot_of(key, part):
    folded = jax.random.fold_in(key, 11)
    key_order, key_shift, key_label, key_local = jax.random.split(folded, 4)
    shift_order = jax.vmap(lambda subkey: jax.random.permutation(subkey, REQUESTS_PER_KEY))(jax.random.split(key_order, N_REQ))
    shifts = jax.random.permutation(key_shift, N_REQ)
    relabel = jax.random.permutation(key_label, N_REQ)
    local_order = jax.vmap(lambda subkey: jax.random.permutation(subkey, REQUESTS_PER_KEY))(jax.random.split(key_local, N_REQ))
    sources = jnp.arange(N_REQ, dtype=jnp.int32)[:, None]
    raw_owner = (sources + shifts[shift_order % N_REQ]) % N_REQ
    owners = relabel[raw_owner]
    local_slot = local_order[owners, shift_order]
    return (owners * REQUESTS_PER_KEY + local_slot).reshape(REQUEST_TOTAL).astype(jnp.int32)


def draw_lengths(key, part):
    key_level, key_len, key_pick = jax.random.split(jax.random.fold_in(key, 23), 3)
    levels = jax.random.randint(key_level, (REQUEST_TOTAL,), 0, 5)
    ceiling = jnp.maximum(CACHE_LIMIT // jnp.left_shift(jnp.int32(1), levels), 2)
    drawn_len = jax.random.randint(key_len, (REQUEST_TOTAL,), 2, ceiling + 1)
    chosen = jax.random.randint(key_pick, (), 0, REQUEST_TOTAL)
    return jnp.where(jnp.arange(REQUEST_TOTAL) == chosen, CACHE_LIMIT, drawn_len).astype(jnp.int32)


def draw_tree(key):
    key_path, key_parent = jax.random.split(jax.random.fold_in(key, 37))
    shuffled = jax.vmap(lambda subkey: jax.random.permutation(subkey, TREE_TOKENS - 1))(jax.random.split(key_path, REQUEST_TOTAL)) + 1
    chosen = jnp.sort(shuffled[:, :ACCEPT_LENGTH - 1], axis=1).astype(jnp.int32)
    tail_path = jnp.arange(TREE_TOKENS - ACCEPT_LENGTH + 1, TREE_TOKENS, dtype=jnp.int32)
    chosen = chosen.at[0].set(tail_path)
    accepted_tokens = jnp.concatenate([jnp.zeros((REQUEST_TOTAL, 1), jnp.int32), chosen], axis=1)
    upper_bound = jnp.maximum(jnp.arange(TREE_TOKENS, dtype=jnp.int32), 1)
    parents = jax.random.randint(key_parent, (REQUEST_TOTAL, TREE_TOKENS), 0, upper_bound[None, :]).astype(jnp.int32)
    row_ids = jnp.arange(REQUEST_TOTAL)[:, None]
    parents = parents.at[row_ids, accepted_tokens[:, 1:]].set(accepted_tokens[:, :-1])
    return (parents.astype(jnp.int32), accepted_tokens.astype(jnp.int32))


def draw_parents(key, part):
    return draw_tree(key)[0]


def draw_accepted_tokens(key, part):
    return draw_tree(key)[1]


def draw_cached_key_value(key, part):
    key_base = jax.random.fold_in(jax.random.fold_in(key, 41), 0)
    complete_shape = (REQUEST_TOTAL, CACHE_LIMIT, KEY_VALUE_HEADS, 2 * HEAD_DIM)
    filled = jax.random.truncated_normal(key_base, -5.0, 5.0, complete_shape, jnp.float32)
    return filled.astype(jnp.bfloat16)


def draw_drafts(key, part):
    key_noise, key_col, key_row = jax.random.split(jax.random.fold_in(key, 53), 3)
    column_log = math.log(3.0) * (jnp.arange(MODEL_DIM, dtype=jnp.float32) / MODEL_DIM - 0.5) + jax.random.uniform(key_col, (MODEL_DIM,), jnp.float32, -0.6, 0.6)
    row_log = jax.random.uniform(key_row, (REQUEST_TOTAL, TREE_TOKENS, 1), jnp.float32, -1.15, 1.15)
    noise = jax.random.truncated_normal(key_noise, -5.0, 5.0, (REQUEST_TOTAL, TREE_TOKENS, MODEL_DIM), jnp.float32)
    return (noise * jnp.exp(column_log + row_log)).astype(jnp.bfloat16)


def shard_levels(own_key, shape, shards, smallest, largest):
    factor_of, own = 1.0, jax.random.fold_in(own_key, 6)
    for position, blocks in shards:
        draws = jnp.exp(jax.random.uniform(jax.random.fold_in(own, position), (blocks,), jnp.float32, smallest / len(shards), largest / len(shards)))
        factor_of = factor_of * jnp.repeat(draws, shape[position] // blocks).reshape([-1 if axis == position else 1 for axis in range(len(shape))])
    return factor_of


def centred(key, shape, spread, limit, cuts=(), kind=jnp.bfloat16):
    loudness = shard_levels(key, shape, cuts, -0.22, 0.18) if cuts else 1.0
    values = jax.random.normal(key, shape, jnp.float32) * spread * loudness
    return jnp.minimum(jnp.maximum(values, -limit), limit).astype(kind)


def setup_inputs(seed: int = 0) -> dict:
    streams_of = jax.random.split(jax.random.key(seed), 15)
    drafts = draw_drafts(jax.random.fold_in(streams_of[14], 71), 0)
    slot_of = draw_slot_of(jax.random.fold_in(streams_of[14], 71), 0)
    lengths = draw_lengths(jax.random.fold_in(streams_of[14], 71), 0)
    parents = draw_parents(jax.random.fold_in(streams_of[14], 71), 0)
    accepted_tokens = draw_accepted_tokens(jax.random.fold_in(streams_of[14], 71), 0)
    cached_key_value = draw_cached_key_value(jax.random.fold_in(streams_of[14], 71), 0)
    attn_gain = jnp.clip(1.0 + 0.18 * jax.random.normal(streams_of[6], (MODEL_DIM,), jnp.float32), 0.1, 1.9)
    query_weight = centred(streams_of[7], (MODEL_DIM, QUERY_HEADS * HEAD_DIM), MODEL_DIM ** -0.5, 0.125, ((1, 4),))
    key_value_weight = centred(streams_of[8], (MODEL_DIM, 2 * KEY_VALUE_HEADS * HEAD_DIM), MODEL_DIM ** -0.5, 0.125, ((1, 4),))
    w_out = centred(streams_of[9], (QUERY_HEADS * HEAD_DIM, MODEL_DIM), (QUERY_HEADS * HEAD_DIM) ** -0.5, 0.21875, ((0, 4),))
    mlp_gain = jnp.clip(1.0 + 0.18 * jax.random.normal(streams_of[10], (MODEL_DIM,), jnp.float32), 0.1, 1.9)
    w_gate = centred(streams_of[11], (MODEL_DIM, FFW), MODEL_DIM ** -0.5, 0.125, ((1, 4),))
    w_up = centred(streams_of[12], (MODEL_DIM, FFW), MODEL_DIM ** -0.5, 0.125, ((1, 4),))
    w_down = centred(streams_of[13], (FFW, MODEL_DIM), FFW ** -0.5, 0.125, ((0, 4),))
    return dict(drafts=drafts, slot_of=slot_of, lengths=lengths, parents=parents, accepted_tokens=accepted_tokens, cached_key_value=cached_key_value, attn_gain=attn_gain, query_weight=query_weight, key_value_weight=key_value_weight, w_out=w_out, mlp_gain=mlp_gain, w_gate=w_gate, w_up=w_up, w_down=w_down)


EPS = 1e-06
HIGH = lax.Precision.HIGHEST

def ancestry(tree_links, tokens):
    parent_link = (tree_links[:, :, None] == jnp.arange(tokens, dtype=jnp.int32)[None, None, :]).astype(jnp.float32)
    reachable = jnp.maximum(parent_link, jnp.eye(tokens, dtype=jnp.float32)[None])
    for squaring in range(max(tokens - 1, 1).bit_length()):
        reachable = jnp.minimum(jnp.einsum('rij,rjk->rik', reachable, reachable, precision=HIGH), 1.0)
    return reachable > 0.5

def rounded(values):
    return lax.optimization_barrier(values.astype(jnp.bfloat16)).astype(jnp.float32)

def rms_norm(matrix_rows, norm_gain):
    return matrix_rows * lax.rsqrt(lax.optimization_barrier(jnp.mean(matrix_rows * matrix_rows, axis=-1, keepdims=True)) + EPS) * norm_gain

def reference(drafts, slot_of, lengths, parents, accepted_tokens, cached_key_value, attn_gain, query_weight, key_value_weight, w_out, mlp_gain, w_gate, w_up, w_down):
    sorted_rows = jnp.zeros_like(drafts).at[slot_of].set(drafts)
    score_scale = 1.0 / math.sqrt(HEAD_DIM)
    head_span = QUERY_HEADS * HEAD_DIM // N_MLP
    unit_span = FFW // N_MLP

    def one_owner(packed):
        owner_rows, cache_len, tree_links, chosen, cache_rows = packed
        per_owner_rows = owner_rows.shape[0]
        flat_rows = owner_rows.reshape(per_owner_rows * TREE_TOKENS, MODEL_DIM).astype(jnp.float32)
        normalized_rows = rms_norm(flat_rows, attn_gain).astype(jnp.bfloat16)
        query_rows = jnp.dot(normalized_rows, query_weight, preferred_element_type=jnp.float32).reshape(per_owner_rows, TREE_TOKENS, KEY_VALUE_HEADS, QUERY_HEADS // KEY_VALUE_HEADS, HEAD_DIM)
        new_key_value = jnp.dot(normalized_rows, key_value_weight, preferred_element_type=jnp.float32).astype(jnp.bfloat16).reshape(per_owner_rows, TREE_TOKENS, KEY_VALUE_HEADS, 2 * HEAD_DIM)
        cache_wide = cache_rows.astype(jnp.float32)
        fresh_wide = new_key_value.astype(jnp.float32)
        score_cache = jnp.einsum('rtkgd,rckd->rkgtc', query_rows, cache_wide[..., :HEAD_DIM], precision=HIGH) * score_scale
        live_rows = jnp.arange(CACHE_LIMIT)[None, :] < cache_len[:, None]
        score_cache = jnp.where(live_rows[:, None, None, None, :], score_cache, -jnp.inf)
        score_draft = jnp.einsum('rtkgd,rjkd->rkgtj', query_rows, fresh_wide[..., :HEAD_DIM], precision=HIGH) * score_scale
        score_draft = jnp.where(ancestry(tree_links, TREE_TOKENS)[:, None, None], score_draft, -jnp.inf)
        row_top = jnp.maximum(lax.optimization_barrier(jnp.max(score_cache, axis=-1)), lax.optimization_barrier(jnp.max(score_draft, axis=-1)))
        weight_cache = rounded(jnp.exp(score_cache - row_top[..., None]))
        weight_draft = rounded(jnp.exp(score_draft - row_top[..., None]))
        numerator = jnp.einsum('rkgtc,rckd->rtkgd', weight_cache, cache_wide[..., HEAD_DIM:], precision=HIGH)
        numerator = numerator + jnp.einsum('rkgtj,rjkd->rtkgd', weight_draft, fresh_wide[..., HEAD_DIM:], precision=HIGH)
        denominator = lax.optimization_barrier(jnp.sum(weight_cache, axis=-1)) + lax.optimization_barrier(jnp.sum(weight_draft, axis=-1))
        attended = (numerator / jnp.transpose(denominator, (0, 3, 1, 2))[..., None]).astype(jnp.bfloat16)
        attended = attended.reshape(per_owner_rows * TREE_TOKENS, QUERY_HEADS * HEAD_DIM)
        attn_sum = jnp.zeros((per_owner_rows * TREE_TOKENS, MODEL_DIM), jnp.float32)
        for group_index in range(N_MLP):
            lower = group_index * head_span
            attn_sum = attn_sum + rounded(jnp.dot(attended[:, lower:lower + head_span], w_out[lower:lower + head_span], preferred_element_type=jnp.float32))
        residual = flat_rows + attn_sum
        normed_two = rms_norm(residual, mlp_gain).astype(jnp.bfloat16)
        gate_out = jnp.dot(normed_two, w_gate, preferred_element_type=jnp.float32)
        up_out = jnp.dot(normed_two, w_up, preferred_element_type=jnp.float32)
        hidden = (jax.nn.silu(gate_out) * up_out).astype(jnp.bfloat16)
        unit_total = jnp.zeros((per_owner_rows * TREE_TOKENS, MODEL_DIM), jnp.float32)
        for group_index in range(N_MLP):
            lower = group_index * unit_span
            unit_total = unit_total + rounded(jnp.dot(hidden[:, lower:lower + unit_span], w_down[lower:lower + unit_span], preferred_element_type=jnp.float32))
        out_rows = (residual + unit_total).astype(jnp.bfloat16).reshape(per_owner_rows, TREE_TOKENS, MODEL_DIM)
        picker = (chosen[:, :, None] == jnp.arange(TREE_TOKENS, dtype=jnp.int32)[None, None, :]).astype(jnp.float32)
        accepted_rows = jnp.einsum('rat,rtkd->rakd', picker, fresh_wide, precision=HIGH).astype(jnp.bfloat16)
        return (out_rows, accepted_rows)
    packed_everything = (sorted_rows.reshape(N_REQ, REQUESTS_PER_KEY, TREE_TOKENS, MODEL_DIM), lengths.reshape(N_REQ, REQUESTS_PER_KEY), parents.reshape(N_REQ, REQUESTS_PER_KEY, TREE_TOKENS), accepted_tokens.reshape(N_REQ, REQUESTS_PER_KEY, ACCEPT_LENGTH), cached_key_value.reshape(N_REQ, REQUESTS_PER_KEY, CACHE_LIMIT, KEY_VALUE_HEADS, 2 * HEAD_DIM))
    out_rows, accepted_rows = lax.map(one_owner, packed_everything)
    owner_out = out_rows.reshape(REQUEST_TOTAL, TREE_TOKENS, MODEL_DIM)
    layer_output = owner_out[slot_of]
    return (layer_output, accepted_rows.reshape(REQUEST_TOTAL, ACCEPT_LENGTH, KEY_VALUE_HEADS, 2 * HEAD_DIM))
```

```python
import math

import jax
import jax.numpy as jnp
from jax import lax
from jax.sharding import PartitionSpec as P

HEAD_DIM = 64


EPS = 1e-06
HIGH = lax.Precision.HIGHEST


def ancestry(tree_links, tokens):
    parent_link = (
        tree_links[:, :, None] == jnp.arange(tokens, dtype=jnp.int32)[None, None, :]
    ).astype(jnp.float32)
    reachable = jnp.maximum(parent_link, jnp.eye(tokens, dtype=jnp.float32)[None])
    for squaring in range(max(tokens - 1, 1).bit_length()):
        reachable = jnp.minimum(
            jnp.einsum("rij,rjk->rik", reachable, reachable, precision=HIGH), 1.0
        )
    return reachable > 0.5


def shift_mlp(value, shift, count):
    return lax.ppermute(value, "mlp", [(i, (i + shift) % count) for i in range(count)])


def gather_mlp(value, count, part_index):
    pieces = [value] + [shift_mlp(value, k, count) for k in range(1, count)]
    stacked = jnp.stack(pieces)
    order = (part_index - jnp.arange(count, dtype=jnp.int32)) % count
    return jnp.take(stacked, order, axis=0, mode="clip")


def per_device(
    drafts,
    slot_of,
    lengths,
    parents,
    accepted_tokens,
    cached_key_value,
    attn_gain,
    query_weight,
    key_value_weight,
    w_out,
    mlp_gain,
    w_gate,
    w_up,
    w_down,
):
    req_count = lax.axis_size("req")
    mlp_count = lax.axis_size("mlp")
    my_index = lax.axis_index("req")
    part_index = lax.axis_index("mlp")
    per_owner_rows, tokens, quarter = drafts.shape
    model_dim = quarter * mlp_count

    w_out_all = gather_mlp(w_out, mlp_count, part_index)

    local_ids = jnp.arange(per_owner_rows, dtype=jnp.int32)
    devices = jnp.arange(req_count, dtype=jnp.int32)
    my_slots = lax.dynamic_slice_in_dim(slot_of, my_index * per_owner_rows, per_owner_rows)
    my_owners = my_slots // per_owner_rows
    send_pick = jnp.sum(
        jnp.where(my_owners[None, :] == devices[:, None], local_ids[None, :], 0), axis=1
    )
    owned_slots = my_index * per_owner_rows + local_ids
    requests = jnp.arange(slot_of.shape[0], dtype=jnp.int32)
    request_of = jnp.sum(
        jnp.where(slot_of[None, :] == owned_slots[:, None], requests[None, :], 0), axis=1
    )
    source_of = request_of // per_owner_rows
    return_pick = jnp.sum(
        jnp.where(source_of[None, :] == devices[:, None], local_ids[None, :], 0), axis=1
    )

    outgoing = jnp.take(drafts, send_pick, axis=0, mode="clip")
    incoming = lax.all_to_all(outgoing, "req", 0, 0, tiled=True)
    local_rows = jnp.take(incoming, source_of, axis=0, mode="clip")

    rows = per_owner_rows * tokens
    full_rows = gather_mlp(local_rows.reshape(rows, quarter), mlp_count, part_index)
    wide_rows = full_rows.astype(jnp.float32)
    square_mean = jnp.sum(wide_rows * wide_rows, axis=(0, 2)) / model_dim
    attn_scale = lax.rsqrt(square_mean + EPS)
    normalized_rows = (
        wide_rows * attn_scale[None, :, None] * attn_gain.reshape(mlp_count, 1, quarter)
    ).astype(jnp.bfloat16)
    kv_heads = key_value_weight.shape[1] // (2 * HEAD_DIM)
    group_heads = query_weight.shape[1] // (kv_heads * HEAD_DIM)
    query_rows = jnp.einsum(
        "jtf,jfc->tc",
        normalized_rows,
        query_weight.reshape(mlp_count, quarter, -1),
        preferred_element_type=jnp.float32,
    ).reshape(per_owner_rows, tokens, kv_heads, group_heads, HEAD_DIM)
    new_key_value = (
        jnp.einsum(
            "jtf,jfc->tc",
            normalized_rows,
            key_value_weight.reshape(mlp_count, quarter, -1),
            preferred_element_type=jnp.float32,
        )
        .astype(jnp.bfloat16)
        .reshape(per_owner_rows, tokens, kv_heads, 2 * HEAD_DIM)
    )
    picker = (
        accepted_tokens[:, :, None] == jnp.arange(tokens, dtype=jnp.int32)[None, None, :]
    ).astype(jnp.bfloat16)
    accepted_rows = jnp.einsum(
        "rat,rtkd->rakd", picker, new_key_value, preferred_element_type=jnp.float32
    ).astype(jnp.bfloat16)

    score_scale = 1.0 / math.sqrt(HEAD_DIM)
    draft_keys = new_key_value[..., :HEAD_DIM].astype(jnp.float32)
    draft_scores = (
        jnp.einsum("rtkgd,rjkd->rkgtj", query_rows, draft_keys, precision=HIGH) * score_scale
    )
    draft_scores = jnp.where(ancestry(parents, tokens)[:, None, None], draft_scores, -jnp.inf)
    draft_top = jnp.max(draft_scores, axis=-1)
    cache_keys = cached_key_value[..., :HEAD_DIM].astype(jnp.float32)
    scores = (
        jnp.einsum("rtkgd,rckd->rkgtc", query_rows, cache_keys, precision=HIGH) * score_scale
    )
    live_rows = jnp.arange(cached_key_value.shape[1])[None, :] < lengths[:, None]
    scores = jnp.where(live_rows[:, None, None, None, :], scores, -jnp.inf)
    row_top = jnp.maximum(draft_top, jnp.max(scores, axis=-1))
    weights = jnp.exp(scores - row_top[..., None]).astype(jnp.bfloat16)
    numerator = jnp.einsum(
        "rkgtc,rckd->rtkgd",
        weights,
        cached_key_value[..., HEAD_DIM:],
        preferred_element_type=jnp.float32,
    )
    denominator = jnp.sum(weights.astype(jnp.float32), axis=-1)
    draft_weights = jnp.exp(draft_scores - row_top[..., None]).astype(jnp.bfloat16)
    numerator = numerator + jnp.einsum(
        "rkgtj,rjkd->rtkgd",
        draft_weights,
        new_key_value[..., HEAD_DIM:],
        preferred_element_type=jnp.float32,
    )
    denominator = denominator + jnp.sum(draft_weights.astype(jnp.float32), axis=-1)
    attended = (numerator / jnp.transpose(denominator, (0, 3, 1, 2))[..., None]).astype(
        jnp.bfloat16
    )
    head_width = kv_heads * group_heads * HEAD_DIM
    attended = attended.reshape(per_owner_rows, tokens, head_width)

    returning = jnp.take(attended, return_pick, axis=0, mode="clip")
    arrived = lax.all_to_all(returning, "req", 0, 0, tiled=True)
    back_rows = jnp.take(arrived, my_owners, axis=0, mode="clip")

    packed = jnp.concatenate(
        [back_rows.reshape(rows, head_width), drafts.reshape(rows, quarter)], axis=1
    )
    gathered = gather_mlp(packed, mlp_count, part_index)
    heads_all = gathered[:, :, :head_width]
    owned_all = gathered[:, :, head_width:].astype(jnp.float32)

    group_products = jnp.einsum(
        "jtc,jcd->jtd", heads_all, w_out_all, preferred_element_type=jnp.float32
    )
    attn_sum = jnp.sum(group_products.astype(jnp.bfloat16).astype(jnp.float32), axis=0)
    residual = jnp.transpose(owned_all, (1, 0, 2)).reshape(rows, model_dim) + attn_sum
    normed_two = (
        residual * lax.rsqrt(jnp.mean(residual * residual, axis=1, keepdims=True) + EPS) * mlp_gain
    ).astype(jnp.bfloat16)
    gate_out = jnp.dot(normed_two, w_gate, preferred_element_type=jnp.float32)
    up_out = jnp.dot(normed_two, w_up, preferred_element_type=jnp.float32)
    hidden = (jax.nn.silu(gate_out) * up_out).astype(jnp.bfloat16)
    unit_part = (
        jnp.dot(hidden, w_down, preferred_element_type=jnp.float32)
        .astype(jnp.bfloat16)
        .reshape(rows, mlp_count, quarter)
    )

    unit_share = lax.dynamic_index_in_dim(unit_part, part_index, 1, keepdims=False).astype(
        jnp.float32
    )
    for k in range(1, mlp_count):
        target = (part_index + k) % mlp_count
        piece = lax.dynamic_index_in_dim(unit_part, target, 1, keepdims=False)
        unit_share = unit_share + shift_mlp(piece, k, mlp_count).astype(jnp.float32)
    residual_share = lax.dynamic_slice_in_dim(residual, part_index * quarter, quarter, 1)
    result = (residual_share + unit_share).astype(jnp.bfloat16)
    return (result.reshape(per_owner_rows, tokens, quarter), accepted_rows)


def solution(mesh):
    placed = (
        P("req", None, "mlp"),
        P(),
        P("req"),
        P("req", None),
        P("req", None),
        P("req", None, "mlp", None),
        P(),
        P(None, "mlp"),
        P(None, "mlp"),
        P("mlp", None),
        P(),
        P(None, "mlp"),
        P(None, "mlp"),
        P("mlp", None),
    )
    return jax.shard_map(
        per_device,
        mesh=mesh,
        in_specs=placed,
        out_specs=(P("req", None, "mlp"), P("req", None, "mlp", None)),
        check_vma=False,
    )
```

```python
import math

import jax
import jax.numpy as jnp
from jax import lax
from jax.sharding import PartitionSpec as P


HEAD_DIM = 64


EPS = 1e-06
HIGH = lax.Precision.HIGHEST


def ancestry(tree_links, tokens):
    parent_link = (
        tree_links[:, :, None] == jnp.arange(tokens, dtype=jnp.int32)[None, None, :]
    ).astype(jnp.float32)
    reachable = jnp.maximum(parent_link, jnp.eye(tokens, dtype=jnp.float32)[None])
    for _ in range(max(tokens - 1, 1).bit_length()):
        reachable = jnp.minimum(
            jnp.einsum("rij,rjk->rik", reachable, reachable, precision=HIGH), 1.0
        )
    return reachable > 0.5


def shift_mlp(value, shift, count):
    return lax.ppermute(value, "mlp", [(i, (i + shift) % count) for i in range(count)])


def stack_mlp(value, count):
    return jnp.stack([value] + [shift_mlp(value, k, count) for k in range(1, count)])


def place_blocks(stacked, count, part_index):
    width = stacked.shape[-1]
    full = jnp.zeros(stacked.shape[1:-1] + (width * count,), stacked.dtype)
    for k in range(count):
        offset = ((part_index - k) % count) * width
        full = lax.dynamic_update_slice_in_dim(full, stacked[k], offset, full.ndim - 1)
    return full


def per_device(
    drafts,
    slot_of,
    lengths,
    parents,
    accepted_tokens,
    cached_key_value,
    attn_gain,
    query_weight,
    key_value_weight,
    w_out,
    mlp_gain,
    w_gate,
    w_up,
    w_down,
):
    req_count = lax.axis_size("req")
    mlp_count = lax.axis_size("mlp")
    my_index = lax.axis_index("req")
    part_index = lax.axis_index("mlp")
    per_owner_rows, tokens, quarter = drafts.shape

    w_out_all = stack_mlp(w_out, mlp_count)

    local_ids = jnp.arange(per_owner_rows, dtype=jnp.int32)
    devices = jnp.arange(req_count, dtype=jnp.int32)
    my_slots = lax.dynamic_slice_in_dim(slot_of, my_index * per_owner_rows, per_owner_rows)
    my_owners = my_slots // per_owner_rows
    send_pick = jnp.sum(
        jnp.where(my_owners[None, :] == devices[:, None], local_ids[None, :], 0), axis=1
    )
    owned_slots = my_index * per_owner_rows + local_ids
    requests = jnp.arange(slot_of.shape[0], dtype=jnp.int32)
    request_of = jnp.sum(
        jnp.where(slot_of[None, :] == owned_slots[:, None], requests[None, :], 0), axis=1
    )
    source_of = request_of // per_owner_rows
    return_pick = jnp.sum(
        jnp.where(source_of[None, :] == devices[:, None], local_ids[None, :], 0), axis=1
    )

    outgoing = jnp.take(drafts, send_pick, axis=0, mode="clip")
    incoming = lax.all_to_all(outgoing, "req", 0, 0, tiled=True)
    local_rows = jnp.take(incoming, source_of, axis=0, mode="clip")

    rows = per_owner_rows * tokens
    full_rows = place_blocks(
        stack_mlp(local_rows.reshape(rows, quarter), mlp_count), mlp_count, part_index
    )
    wide_rows = full_rows.astype(jnp.float32)
    normalized_rows = (
        wide_rows
        * lax.rsqrt(jnp.mean(wide_rows * wide_rows, axis=1, keepdims=True) + EPS)
        * attn_gain
    ).astype(jnp.bfloat16)
    kv_heads = key_value_weight.shape[1] // (2 * HEAD_DIM)
    group_heads = query_weight.shape[1] // (kv_heads * HEAD_DIM)
    query_rows = jnp.dot(normalized_rows, query_weight, preferred_element_type=jnp.float32).reshape(
        per_owner_rows, tokens, kv_heads, group_heads, HEAD_DIM
    )
    new_key_value = (
        jnp.dot(normalized_rows, key_value_weight, preferred_element_type=jnp.float32)
        .astype(jnp.bfloat16)
        .reshape(per_owner_rows, tokens, kv_heads, 2 * HEAD_DIM)
    )
    picker = (
        accepted_tokens[:, :, None] == jnp.arange(tokens, dtype=jnp.int32)[None, None, :]
    ).astype(jnp.bfloat16)
    accepted_rows = jnp.einsum(
        "rat,rtkd->rakd", picker, new_key_value, preferred_element_type=jnp.float32
    ).astype(jnp.bfloat16)

    score_scale = 1.0 / math.sqrt(HEAD_DIM)
    draft_keys = new_key_value[..., :HEAD_DIM].astype(jnp.float32)
    draft_scores = (
        jnp.einsum("rtkgd,rjkd->rkgtj", query_rows, draft_keys, precision=HIGH) * score_scale
    )
    draft_scores = jnp.where(ancestry(parents, tokens)[:, None, None], draft_scores, -jnp.inf)
    draft_top = jnp.max(draft_scores, axis=-1)
    cache_keys = cached_key_value[..., :HEAD_DIM].astype(jnp.float32)
    scores = (
        jnp.einsum("rtkgd,rckd->rkgtc", query_rows, cache_keys, precision=HIGH) * score_scale
    )
    live_rows = jnp.arange(cached_key_value.shape[1])[None, :] < lengths[:, None]
    scores = jnp.where(live_rows[:, None, None, None, :], scores, -jnp.inf)
    row_top = jnp.maximum(draft_top, jnp.max(scores, axis=-1))
    weights = jnp.exp(scores - row_top[..., None]).astype(jnp.bfloat16)
    numerator = jnp.einsum(
        "rkgtc,rckd->rtkgd",
        weights,
        cached_key_value[..., HEAD_DIM:],
        preferred_element_type=jnp.float32,
    )
    denominator = jnp.sum(weights.astype(jnp.float32), axis=-1)
    draft_weights = jnp.exp(draft_scores - row_top[..., None]).astype(jnp.bfloat16)
    numerator = numerator + jnp.einsum(
        "rkgtj,rjkd->rtkgd",
        draft_weights,
        new_key_value[..., HEAD_DIM:],
        preferred_element_type=jnp.float32,
    )
    denominator = denominator + jnp.sum(draft_weights.astype(jnp.float32), axis=-1)
    attended = (numerator / jnp.transpose(denominator, (0, 3, 1, 2))[..., None]).astype(
        jnp.bfloat16
    )
    head_width = kv_heads * group_heads * HEAD_DIM
    attended = attended.reshape(per_owner_rows, tokens, head_width)

    returning = jnp.take(attended, return_pick, axis=0, mode="clip")
    arrived = lax.all_to_all(returning, "req", 0, 0, tiled=True)
    back_rows = jnp.take(arrived, my_owners, axis=0, mode="clip")

    packed = jnp.concatenate(
        [back_rows.reshape(rows, head_width), drafts.reshape(rows, quarter)], axis=1
    )
    gathered = stack_mlp(packed, mlp_count)
    heads_all = gathered[:, :, :head_width]
    owned_all = place_blocks(gathered[:, :, head_width:], mlp_count, part_index)

    group_products = jnp.einsum(
        "jtc,jcd->jtd", heads_all, w_out_all, preferred_element_type=jnp.float32
    )
    attn_sum = jnp.sum(group_products.astype(jnp.bfloat16).astype(jnp.float32), axis=0)
    residual = owned_all.astype(jnp.float32) + attn_sum
    normed_two = (
        residual * lax.rsqrt(jnp.mean(residual * residual, axis=1, keepdims=True) + EPS) * mlp_gain
    ).astype(jnp.bfloat16)
    gate_out = jnp.dot(normed_two, w_gate, preferred_element_type=jnp.float32)
    up_out = jnp.dot(normed_two, w_up, preferred_element_type=jnp.float32)
    hidden = (jax.nn.silu(gate_out) * up_out).astype(jnp.bfloat16)
    unit_part = jnp.einsum(
        "tu,ujd->jtd",
        hidden,
        w_down.reshape(w_down.shape[0], mlp_count, quarter),
        preferred_element_type=jnp.float32,
    ).astype(jnp.bfloat16)

    unit_share = lax.dynamic_index_in_dim(unit_part, part_index, 0, keepdims=False).astype(
        jnp.float32
    )
    for k in range(1, mlp_count):
        target = (part_index + k) % mlp_count
        piece = lax.dynamic_index_in_dim(unit_part, target, 0, keepdims=False)
        unit_share = unit_share + shift_mlp(piece, k, mlp_count).astype(jnp.float32)
    residual_share = lax.dynamic_slice_in_dim(residual, part_index * quarter, quarter, 1)
    result = (residual_share + unit_share).astype(jnp.bfloat16)
    return (result.reshape(per_owner_rows, tokens, quarter), accepted_rows)


def solution(mesh):
    placed = (
        P("req", None, "mlp"),
        P(),
        P("req"),
        P("req", None),
        P("req", None),
        P("req", None, "mlp", None),
        P(),
        P(None, "mlp"),
        P(None, "mlp"),
        P("mlp", None),
        P(),
        P(None, "mlp"),
        P(None, "mlp"),
        P("mlp", None),
    )
    return jax.shard_map(
        per_device,
        mesh=mesh,
        in_specs=placed,
        out_specs=(P("req", None, "mlp"), P("req", None, "mlp", None)),
        check_vma=False,
    )
```

```python
import math

import jax
import jax.numpy as jnp
from jax import lax
from jax.sharding import PartitionSpec as P


HEAD_DIM = 64


EPS = 1e-06
HIGH = lax.Precision.HIGHEST


def ancestry(tree_links, tokens):
    parent_link = (
        tree_links[:, :, None] == jnp.arange(tokens, dtype=jnp.int32)[None, None, :]
    ).astype(jnp.float32)
    reachable = jnp.maximum(parent_link, jnp.eye(tokens, dtype=jnp.float32)[None])
    for _ in range(max(tokens - 1, 1).bit_length()):
        reachable = jnp.minimum(
            jnp.einsum("rij,rjk->rik", reachable, reachable, precision=HIGH), 1.0
        )
    return reachable > 0.5


def shift_mlp(value, shift, count):
    return lax.ppermute(value, "mlp", [(i, (i + shift) % count) for i in range(count)])


def pieces_mlp(value, count):
    return [value] + [shift_mlp(value, k, count) for k in range(1, count)]


def place_blocks(pieces, count, part_index):
    width = pieces[0].shape[-1]
    full = jnp.zeros(pieces[0].shape[:-1] + (width * count,), pieces[0].dtype)
    for k, piece in enumerate(pieces):
        offset = ((part_index - k) % count) * width
        full = lax.dynamic_update_slice_in_dim(full, piece, offset, full.ndim - 1)
    return full


def per_device(
    drafts,
    slot_of,
    lengths,
    parents,
    accepted_tokens,
    cached_key_value,
    attn_gain,
    query_weight,
    key_value_weight,
    w_out,
    mlp_gain,
    w_gate,
    w_up,
    w_down,
):
    req_count = lax.axis_size("req")
    mlp_count = lax.axis_size("mlp")
    my_index = lax.axis_index("req")
    part_index = lax.axis_index("mlp")
    per_owner_rows, tokens, quarter = drafts.shape

    w_out_all = pieces_mlp(w_out, mlp_count)

    local_ids = jnp.arange(per_owner_rows, dtype=jnp.int32)
    devices = jnp.arange(req_count, dtype=jnp.int32)
    my_slots = lax.dynamic_slice_in_dim(slot_of, my_index * per_owner_rows, per_owner_rows)
    my_owners = my_slots // per_owner_rows
    send_pick = jnp.sum(
        jnp.where(my_owners[None, :] == devices[:, None], local_ids[None, :], 0), axis=1
    )
    owned_slots = my_index * per_owner_rows + local_ids
    requests = jnp.arange(slot_of.shape[0], dtype=jnp.int32)
    request_of = jnp.sum(
        jnp.where(slot_of[None, :] == owned_slots[:, None], requests[None, :], 0), axis=1
    )
    source_of = request_of // per_owner_rows
    return_pick = jnp.sum(
        jnp.where(source_of[None, :] == devices[:, None], local_ids[None, :], 0), axis=1
    )

    outgoing = jnp.take(drafts, send_pick, axis=0, mode="clip")
    incoming = lax.all_to_all(outgoing, "req", 0, 0, tiled=True)
    local_rows = jnp.take(incoming, source_of, axis=0, mode="clip")

    rows = per_owner_rows * tokens
    full_rows = place_blocks(
        pieces_mlp(local_rows.reshape(rows, quarter), mlp_count), mlp_count, part_index
    )
    wide_rows = full_rows.astype(jnp.float32)
    normalized_rows = (
        wide_rows
        * lax.rsqrt(jnp.mean(wide_rows * wide_rows, axis=1, keepdims=True) + EPS)
        * attn_gain
    ).astype(jnp.bfloat16)
    kv_heads = key_value_weight.shape[1] // (2 * HEAD_DIM)
    group_heads = query_weight.shape[1] // (kv_heads * HEAD_DIM)
    query_rows = jnp.dot(normalized_rows, query_weight, preferred_element_type=jnp.float32).reshape(
        per_owner_rows, tokens, kv_heads, group_heads, HEAD_DIM
    )
    new_key_value = (
        jnp.dot(normalized_rows, key_value_weight, preferred_element_type=jnp.float32)
        .astype(jnp.bfloat16)
        .reshape(per_owner_rows, tokens, kv_heads, 2 * HEAD_DIM)
    )
    picker = (
        accepted_tokens[:, :, None] == jnp.arange(tokens, dtype=jnp.int32)[None, None, :]
    ).astype(jnp.bfloat16)
    accepted_rows = jnp.einsum(
        "rat,rtkd->rakd", picker, new_key_value, preferred_element_type=jnp.float32
    ).astype(jnp.bfloat16)

    score_scale = 1.0 / math.sqrt(HEAD_DIM)
    draft_keys = new_key_value[..., :HEAD_DIM].astype(jnp.float32)
    draft_scores = (
        jnp.einsum("rtkgd,rjkd->rkgtj", query_rows, draft_keys, precision=HIGH) * score_scale
    )
    draft_scores = jnp.where(ancestry(parents, tokens)[:, None, None], draft_scores, -jnp.inf)
    draft_top = jnp.max(draft_scores, axis=-1)
    cache_keys = cached_key_value[..., :HEAD_DIM].astype(jnp.float32)
    scores = (
        jnp.einsum("rtkgd,rckd->rkgtc", query_rows, cache_keys, precision=HIGH) * score_scale
    )
    live_rows = jnp.arange(cached_key_value.shape[1])[None, :] < lengths[:, None]
    scores = jnp.where(live_rows[:, None, None, None, :], scores, -jnp.inf)
    row_top = jnp.maximum(draft_top, jnp.max(scores, axis=-1))
    weights = jnp.exp(scores - row_top[..., None]).astype(jnp.bfloat16)
    numerator = jnp.einsum(
        "rkgtc,rckd->rtkgd",
        weights,
        cached_key_value[..., HEAD_DIM:],
        preferred_element_type=jnp.float32,
    )
    denominator = jnp.sum(weights.astype(jnp.float32), axis=-1)
    draft_weights = jnp.exp(draft_scores - row_top[..., None]).astype(jnp.bfloat16)
    numerator = numerator + jnp.einsum(
        "rkgtj,rjkd->rtkgd",
        draft_weights,
        new_key_value[..., HEAD_DIM:],
        preferred_element_type=jnp.float32,
    )
    denominator = denominator + jnp.sum(draft_weights.astype(jnp.float32), axis=-1)
    attended = (numerator / jnp.transpose(denominator, (0, 3, 1, 2))[..., None]).astype(
        jnp.bfloat16
    )
    head_width = kv_heads * group_heads * HEAD_DIM
    attended = attended.reshape(per_owner_rows, tokens, head_width)

    returning = jnp.take(attended, return_pick, axis=0, mode="clip")
    arrived = lax.all_to_all(returning, "req", 0, 0, tiled=True)
    back_rows = jnp.take(arrived, my_owners, axis=0, mode="clip")

    packed = jnp.concatenate(
        [drafts.reshape(rows, quarter), back_rows.reshape(rows, head_width)], axis=1
    )
    gathered = pieces_mlp(packed, mlp_count)
    owned_all = place_blocks([piece[:, :quarter] for piece in gathered], mlp_count, part_index)

    residual = owned_all.astype(jnp.float32)
    for piece, rows_of_group in zip(gathered, w_out_all):
        group_product = jnp.dot(
            piece[:, quarter:], rows_of_group, preferred_element_type=jnp.float32
        )
        residual = residual + group_product.astype(jnp.bfloat16).astype(jnp.float32)
    normed_two = (
        residual * lax.rsqrt(jnp.mean(residual * residual, axis=1, keepdims=True) + EPS) * mlp_gain
    ).astype(jnp.bfloat16)
    gate_out = jnp.dot(normed_two, w_gate, preferred_element_type=jnp.float32)
    up_out = jnp.dot(normed_two, w_up, preferred_element_type=jnp.float32)
    hidden = (jax.nn.silu(gate_out) * up_out).astype(jnp.bfloat16)
    unit_part = jnp.einsum(
        "tu,ujd->jtd",
        hidden,
        w_down.reshape(w_down.shape[0], mlp_count, quarter),
        preferred_element_type=jnp.float32,
    ).astype(jnp.bfloat16)

    unit_share = lax.dynamic_index_in_dim(unit_part, part_index, 0, keepdims=False).astype(
        jnp.float32
    )
    for k in range(1, mlp_count):
        target = (part_index + k) % mlp_count
        piece = lax.dynamic_index_in_dim(unit_part, target, 0, keepdims=False)
        unit_share = unit_share + shift_mlp(piece, k, mlp_count).astype(jnp.float32)
    residual_share = lax.dynamic_slice_in_dim(residual, part_index * quarter, quarter, 1)
    result = (residual_share + unit_share).astype(jnp.bfloat16)
    return (result.reshape(per_owner_rows, tokens, quarter), accepted_rows)


def solution(mesh):
    placed = (
        P("req", None, "mlp"),
        P(),
        P("req"),
        P("req", None),
        P("req", None),
        P("req", None, "mlp", None),
        P(),
        P(None, "mlp"),
        P(None, "mlp"),
        P("mlp", None),
        P(),
        P(None, "mlp"),
        P(None, "mlp"),
        P("mlp", None),
    )
    return jax.shard_map(
        per_device,
        mesh=mesh,
        in_specs=placed,
        out_specs=(P("req", None, "mlp"), P("req", None, "mlp", None)),
        check_vma=False,
    )
```

```python
import math

import jax
import jax.numpy as jnp
from jax import lax
from jax.sharding import PartitionSpec as P


HEAD_DIM = 64


EPS = 1e-06
HIGH = lax.Precision.HIGHEST


def ancestry(tree_links, tokens):
    parent_link = (
        tree_links[:, :, None] == jnp.arange(tokens, dtype=jnp.int32)[None, None, :]
    ).astype(jnp.float32)
    reachable = jnp.maximum(parent_link, jnp.eye(tokens, dtype=jnp.float32)[None])
    for _ in range(max(tokens - 1, 1).bit_length()):
        reachable = jnp.minimum(
            jnp.einsum("rij,rjk->rik", reachable, reachable, precision=HIGH), 1.0
        )
    return reachable > 0.5


def shift_mlp(value, shift, count):
    return lax.ppermute(value, "mlp", [(i, (i + shift) % count) for i in range(count)])


def pieces_mlp(value, count):
    return [value] + [shift_mlp(value, k, count) for k in range(1, count)]


def place_blocks(pieces, count, part_index):
    width = pieces[0].shape[-1]
    full = jnp.zeros(pieces[0].shape[:-1] + (width * count,), pieces[0].dtype)
    for k, piece in enumerate(pieces):
        offset = ((part_index - k) % count) * width
        full = lax.dynamic_update_slice_in_dim(full, piece, offset, full.ndim - 1)
    return full


def per_device(
    drafts,
    slot_of,
    lengths,
    parents,
    accepted_tokens,
    cached_key_value,
    attn_gain,
    query_weight,
    key_value_weight,
    w_out,
    mlp_gain,
    w_gate,
    w_up,
    w_down,
):
    req_count = lax.axis_size("req")
    mlp_count = lax.axis_size("mlp")
    my_index = lax.axis_index("req")
    part_index = lax.axis_index("mlp")
    per_owner_rows, tokens, quarter = drafts.shape

    w_out_all = pieces_mlp(w_out, mlp_count)

    local_ids = jnp.arange(per_owner_rows, dtype=jnp.int32)
    devices = jnp.arange(req_count, dtype=jnp.int32)
    my_slots = lax.dynamic_slice_in_dim(slot_of, my_index * per_owner_rows, per_owner_rows)
    my_owners = my_slots // per_owner_rows
    send_pick = jnp.sum(
        jnp.where(my_owners[None, :] == devices[:, None], local_ids[None, :], 0), axis=1
    )
    owned_slots = my_index * per_owner_rows + local_ids
    requests = jnp.arange(slot_of.shape[0], dtype=jnp.int32)
    request_of = jnp.sum(
        jnp.where(slot_of[None, :] == owned_slots[:, None], requests[None, :], 0), axis=1
    )
    source_of = request_of // per_owner_rows
    return_pick = jnp.sum(
        jnp.where(source_of[None, :] == devices[:, None], local_ids[None, :], 0), axis=1
    )

    outgoing = jnp.take(drafts, send_pick, axis=0, mode="clip")
    incoming = lax.all_to_all(outgoing, "req", 0, 0, tiled=True)
    local_rows = jnp.take(incoming, source_of, axis=0, mode="clip")

    rows = per_owner_rows * tokens
    owner_pieces = pieces_mlp(local_rows.reshape(rows, quarter), mlp_count)
    full_rows = place_blocks(owner_pieces, mlp_count, part_index)
    wide_rows = full_rows.astype(jnp.float32)
    normalized_rows = (
        wide_rows
        * lax.rsqrt(jnp.mean(wide_rows * wide_rows, axis=1, keepdims=True) + EPS)
        * attn_gain
    ).astype(jnp.bfloat16)
    kv_heads = key_value_weight.shape[1] // (2 * HEAD_DIM)
    group_heads = query_weight.shape[1] // (kv_heads * HEAD_DIM)
    query_rows = jnp.dot(normalized_rows, query_weight, preferred_element_type=jnp.float32).reshape(
        per_owner_rows, tokens, kv_heads, group_heads, HEAD_DIM
    )
    new_key_value = (
        jnp.dot(normalized_rows, key_value_weight, preferred_element_type=jnp.float32)
        .astype(jnp.bfloat16)
        .reshape(per_owner_rows, tokens, kv_heads, 2 * HEAD_DIM)
    )
    picker = (
        accepted_tokens[:, :, None] == jnp.arange(tokens, dtype=jnp.int32)[None, None, :]
    ).astype(jnp.bfloat16)
    accepted_rows = jnp.einsum(
        "rat,rtkd->rakd", picker, new_key_value, preferred_element_type=jnp.float32
    ).astype(jnp.bfloat16)

    score_scale = 1.0 / math.sqrt(HEAD_DIM)
    draft_keys = new_key_value[..., :HEAD_DIM].astype(jnp.float32)
    draft_scores = (
        jnp.einsum("rtkgd,rjkd->rkgtj", query_rows, draft_keys, precision=HIGH) * score_scale
    )
    draft_scores = jnp.where(ancestry(parents, tokens)[:, None, None], draft_scores, -jnp.inf)
    draft_top = jnp.max(draft_scores, axis=-1)
    cache_keys = cached_key_value[..., :HEAD_DIM].astype(jnp.float32)
    scores = (
        jnp.einsum("rtkgd,rckd->rkgtc", query_rows, cache_keys, precision=HIGH) * score_scale
    )
    live_rows = jnp.arange(cached_key_value.shape[1])[None, :] < lengths[:, None]
    scores = jnp.where(live_rows[:, None, None, None, :], scores, -jnp.inf)
    row_top = jnp.maximum(draft_top, jnp.max(scores, axis=-1))
    weights = jnp.exp(scores - row_top[..., None]).astype(jnp.bfloat16)
    numerator = jnp.einsum(
        "rkgtc,rckd->rtkgd",
        weights,
        cached_key_value[..., HEAD_DIM:],
        preferred_element_type=jnp.float32,
    )
    denominator = jnp.sum(weights.astype(jnp.float32), axis=-1)
    draft_weights = jnp.exp(draft_scores - row_top[..., None]).astype(jnp.bfloat16)
    numerator = numerator + jnp.einsum(
        "rkgtj,rjkd->rtkgd",
        draft_weights,
        new_key_value[..., HEAD_DIM:],
        preferred_element_type=jnp.float32,
    )
    denominator = denominator + jnp.sum(draft_weights.astype(jnp.float32), axis=-1)
    attended = (numerator / jnp.transpose(denominator, (0, 3, 1, 2))[..., None]).astype(
        jnp.bfloat16
    )
    head_width = kv_heads * group_heads * HEAD_DIM
    attended = attended.reshape(per_owner_rows, tokens, head_width)

    returning = jnp.take(attended, return_pick, axis=0, mode="clip")
    arrived = lax.all_to_all(returning, "req", 0, 0, tiled=True)
    back_rows = jnp.take(arrived, my_owners, axis=0, mode="clip")

    packed = jnp.concatenate(
        [drafts.reshape(rows, quarter), back_rows.reshape(rows, head_width)], axis=1
    )
    gathered = pieces_mlp(packed, mlp_count)
    owned_all = place_blocks([piece[:, :quarter] for piece in gathered], mlp_count, part_index)

    residual = owned_all.astype(jnp.float32)
    for piece, rows_of_group in zip(gathered, w_out_all):
        group_product = jnp.dot(
            piece[:, quarter:], rows_of_group, preferred_element_type=jnp.float32
        )
        residual = residual + group_product.astype(jnp.bfloat16).astype(jnp.float32)
    normed_two = (
        residual * lax.rsqrt(jnp.mean(residual * residual, axis=1, keepdims=True) + EPS) * mlp_gain
    ).astype(jnp.bfloat16)
    gate_out = jnp.dot(normed_two, w_gate, preferred_element_type=jnp.float32)
    up_out = jnp.dot(normed_two, w_up, preferred_element_type=jnp.float32)
    hidden = (jax.nn.silu(gate_out) * up_out).astype(jnp.bfloat16)
    unit_part = jnp.einsum(
        "tu,ujd->jtd",
        hidden,
        w_down.reshape(w_down.shape[0], mlp_count, quarter),
        preferred_element_type=jnp.float32,
    ).astype(jnp.bfloat16)

    unit_share = lax.dynamic_index_in_dim(unit_part, part_index, 0, keepdims=False).astype(
        jnp.float32
    )
    for k in range(1, mlp_count):
        target = (part_index + k) % mlp_count
        piece = lax.dynamic_index_in_dim(unit_part, target, 0, keepdims=False)
        unit_share = unit_share + shift_mlp(piece, k, mlp_count).astype(jnp.float32)
    residual_share = lax.dynamic_slice_in_dim(residual, part_index * quarter, quarter, 1)
    result = (residual_share + unit_share).astype(jnp.bfloat16)
    return (result.reshape(per_owner_rows, tokens, quarter), accepted_rows)


def solution(mesh):
    placed = (
        P("req", None, "mlp"),
        P(),
        P("req"),
        P("req", None),
        P("req", None),
        P("req", None, "mlp", None),
        P(),
        P(None, "mlp"),
        P(None, "mlp"),
        P("mlp", None),
        P(),
        P(None, "mlp"),
        P(None, "mlp"),
        P("mlp", None),
    )
    return jax.shard_map(
        per_device,
        mesh=mesh,
        in_specs=placed,
        out_specs=(P("req", None, "mlp"), P("req", None, "mlp", None)),
        check_vma=False,
    )
```

```python
import math

import jax
import jax.numpy as jnp
from jax import lax
from jax.sharding import PartitionSpec as P


HEAD_DIM = 64


EPS = 1e-06
HIGH = lax.Precision.HIGHEST


def ancestry(tree_links, tokens):
    parent_link = (
        tree_links[:, :, None] == jnp.arange(tokens, dtype=jnp.int32)[None, None, :]
    ).astype(jnp.float32)
    reachable = jnp.maximum(parent_link, jnp.eye(tokens, dtype=jnp.float32)[None])
    for _ in range(max(tokens - 1, 1).bit_length()):
        reachable = jnp.minimum(
            jnp.einsum("rij,rjk->rik", reachable, reachable, precision=HIGH), 1.0
        )
    return reachable > 0.5


def shift_mlp(value, shift, count):
    return lax.ppermute(value, "mlp", [(i, (i + shift) % count) for i in range(count)])


def pieces_mlp(value, count):
    return [value] + [shift_mlp(value, k, count) for k in range(1, count)]


def place_blocks(pieces, count, part_index):
    width = pieces[0].shape[-1]
    full = jnp.zeros(pieces[0].shape[:-1] + (width * count,), pieces[0].dtype)
    for k, piece in enumerate(pieces):
        offset = ((part_index - k) % count) * width
        full = lax.dynamic_update_slice_in_dim(full, piece, offset, full.ndim - 1)
    return full


def per_device(
    drafts,
    slot_of,
    lengths,
    parents,
    accepted_tokens,
    cached_key_value,
    attn_gain,
    query_weight,
    key_value_weight,
    w_out,
    mlp_gain,
    w_gate,
    w_up,
    w_down,
):
    req_count = lax.axis_size("req")
    mlp_count = lax.axis_size("mlp")
    my_index = lax.axis_index("req")
    part_index = lax.axis_index("mlp")
    per_owner_rows, tokens, quarter = drafts.shape

    w_out_all = pieces_mlp(w_out, mlp_count)

    local_ids = jnp.arange(per_owner_rows, dtype=jnp.int32)
    devices = jnp.arange(req_count, dtype=jnp.int32)
    my_slots = lax.dynamic_slice_in_dim(slot_of, my_index * per_owner_rows, per_owner_rows)
    my_owners = my_slots // per_owner_rows
    send_pick = jnp.sum(
        jnp.where(my_owners[None, :] == devices[:, None], local_ids[None, :], 0), axis=1
    )
    owned_slots = my_index * per_owner_rows + local_ids
    requests = jnp.arange(slot_of.shape[0], dtype=jnp.int32)
    request_of = jnp.sum(
        jnp.where(slot_of[None, :] == owned_slots[:, None], requests[None, :], 0), axis=1
    )
    source_of = request_of // per_owner_rows
    return_pick = jnp.sum(
        jnp.where(source_of[None, :] == devices[:, None], local_ids[None, :], 0), axis=1
    )

    outgoing = jnp.take(drafts, send_pick, axis=0, mode="clip")
    incoming = lax.all_to_all(outgoing, "req", 0, 0, tiled=True)
    local_rows = jnp.take(incoming, source_of, axis=0, mode="clip")

    rows = per_owner_rows * tokens
    owner_pieces = pieces_mlp(local_rows.reshape(rows, quarter), mlp_count)
    full_rows = place_blocks(owner_pieces, mlp_count, part_index)
    wide_rows = full_rows.astype(jnp.float32)
    normalized_rows = (
        wide_rows
        * lax.rsqrt(jnp.mean(wide_rows * wide_rows, axis=1, keepdims=True) + EPS)
        * attn_gain
    ).astype(jnp.bfloat16)
    kv_heads = key_value_weight.shape[1] // (2 * HEAD_DIM)
    group_heads = query_weight.shape[1] // (kv_heads * HEAD_DIM)
    query_rows = jnp.dot(normalized_rows, query_weight, preferred_element_type=jnp.float32).reshape(
        per_owner_rows, tokens, kv_heads, group_heads, HEAD_DIM
    )
    new_key_value = (
        jnp.dot(normalized_rows, key_value_weight, preferred_element_type=jnp.float32)
        .astype(jnp.bfloat16)
        .reshape(per_owner_rows, tokens, kv_heads, 2 * HEAD_DIM)
    )
    picker = (
        accepted_tokens[:, :, None] == jnp.arange(tokens, dtype=jnp.int32)[None, None, :]
    ).astype(jnp.bfloat16)
    accepted_rows = jnp.einsum(
        "rat,rtkd->rakd", picker, new_key_value, preferred_element_type=jnp.float32
    ).astype(jnp.bfloat16)

    score_scale = 1.0 / math.sqrt(HEAD_DIM)
    draft_keys = new_key_value[..., :HEAD_DIM].astype(jnp.float32)
    draft_scores = (
        jnp.einsum("rtkgd,rjkd->rkgtj", query_rows, draft_keys, precision=HIGH) * score_scale
    )
    draft_scores = jnp.where(ancestry(parents, tokens)[:, None, None], draft_scores, -jnp.inf)
    draft_top = jnp.max(draft_scores, axis=-1)
    cache_keys = cached_key_value[..., :HEAD_DIM].astype(jnp.float32)
    scores = (
        jnp.einsum("rtkgd,rckd->rkgtc", query_rows, cache_keys, precision=HIGH) * score_scale
    )
    live_rows = jnp.arange(cached_key_value.shape[1])[None, :] < lengths[:, None]
    scores = jnp.where(live_rows[:, None, None, None, :], scores, -jnp.inf)
    row_top = jnp.maximum(draft_top, jnp.max(scores, axis=-1))
    weights = jnp.exp(scores - row_top[..., None]).astype(jnp.bfloat16)
    numerator = jnp.einsum(
        "rkgtc,rckd->rtkgd",
        weights,
        cached_key_value[..., HEAD_DIM:],
        preferred_element_type=jnp.float32,
    )
    denominator = jnp.sum(weights.astype(jnp.float32), axis=-1)
    draft_weights = jnp.exp(draft_scores - row_top[..., None]).astype(jnp.bfloat16)
    numerator = numerator + jnp.einsum(
        "rkgtj,rjkd->rtkgd",
        draft_weights,
        new_key_value[..., HEAD_DIM:],
        preferred_element_type=jnp.float32,
    )
    denominator = denominator + jnp.sum(draft_weights.astype(jnp.float32), axis=-1)
    attended = (numerator / jnp.transpose(denominator, (0, 3, 1, 2))[..., None]).astype(
        jnp.bfloat16
    )
    head_width = kv_heads * group_heads * HEAD_DIM
    attended = attended.reshape(per_owner_rows, tokens, head_width)

    returning = jnp.take(attended, return_pick, axis=0, mode="clip")
    arrived = lax.all_to_all(returning, "req", 0, 0, tiled=True)
    back_rows = jnp.take(arrived, my_owners, axis=0, mode="clip")

    packed = jnp.concatenate(
        [drafts.reshape(rows, quarter), back_rows.reshape(rows, head_width)], axis=1
    )
    gathered = pieces_mlp(packed, mlp_count)
    owned_all = place_blocks([piece[:, :quarter] for piece in gathered], mlp_count, part_index)

    residual = owned_all.astype(jnp.float32)
    for piece, rows_of_group in zip(gathered, w_out_all):
        group_product = jnp.dot(
            piece[:, quarter:], rows_of_group, preferred_element_type=jnp.float32
        )
        residual = residual + group_product.astype(jnp.bfloat16).astype(jnp.float32)
    normed_two = (
        residual * lax.rsqrt(jnp.mean(residual * residual, axis=1, keepdims=True) + EPS) * mlp_gain
    ).astype(jnp.bfloat16)
    residual_share = lax.dynamic_slice_in_dim(residual, part_index * quarter, quarter, 1)
    halves = []
    half = rows // 2
    for lower in (0, half):
        normed_half = normed_two[lower : lower + half]
        gate_out = jnp.dot(normed_half, w_gate, preferred_element_type=jnp.float32)
        up_out = jnp.dot(normed_half, w_up, preferred_element_type=jnp.float32)
        hidden = (jax.nn.silu(gate_out) * up_out).astype(jnp.bfloat16)
        unit_part = jnp.einsum(
            "tu,ujd->jtd",
            hidden,
            w_down.reshape(w_down.shape[0], mlp_count, quarter),
            preferred_element_type=jnp.float32,
        ).astype(jnp.bfloat16)

        unit_share = lax.dynamic_index_in_dim(unit_part, part_index, 0, keepdims=False).astype(
            jnp.float32
        )
        for k in range(1, mlp_count):
            target = (part_index + k) % mlp_count
            piece = lax.dynamic_index_in_dim(unit_part, target, 0, keepdims=False)
            unit_share = unit_share + shift_mlp(piece, k, mlp_count).astype(jnp.float32)
        halves.append((residual_share[lower : lower + half] + unit_share).astype(jnp.bfloat16))
    result = jnp.concatenate(halves, axis=0)
    return (result.reshape(per_owner_rows, tokens, quarter), accepted_rows)


def solution(mesh):
    placed = (
        P("req", None, "mlp"),
        P(),
        P("req"),
        P("req", None),
        P("req", None),
        P("req", None, "mlp", None),
        P(),
        P(None, "mlp"),
        P(None, "mlp"),
        P("mlp", None),
        P(),
        P(None, "mlp"),
        P(None, "mlp"),
        P("mlp", None),
    )
    return jax.shard_map(
        per_device,
        mesh=mesh,
        in_specs=placed,
        out_specs=(P("req", None, "mlp"), P("req", None, "mlp", None)),
        check_vma=False,
    )
```

```python
import math

import jax
import jax.numpy as jnp
from jax import lax
from jax.sharding import PartitionSpec as P


HEAD_DIM = 64


EPS = 1e-06
HIGH = lax.Precision.HIGHEST


def ancestry(tree_links, tokens):
    parent_link = (
        tree_links[:, :, None] == jnp.arange(tokens, dtype=jnp.int32)[None, None, :]
    ).astype(jnp.float32)
    reachable = jnp.maximum(parent_link, jnp.eye(tokens, dtype=jnp.float32)[None])
    for _ in range(max(tokens - 1, 1).bit_length()):
        reachable = jnp.minimum(
            jnp.einsum("rij,rjk->rik", reachable, reachable, precision=HIGH), 1.0
        )
    return reachable > 0.5


def shift_mlp(value, shift, count):
    return lax.ppermute(value, "mlp", [(i, (i + shift) % count) for i in range(count)])


def pieces_mlp(value, count):
    return [value] + [shift_mlp(value, k, count) for k in range(1, count)]


def place_blocks(pieces, count, part_index):
    width = pieces[0].shape[-1]
    full = jnp.zeros(pieces[0].shape[:-1] + (width * count,), pieces[0].dtype)
    for k, piece in enumerate(pieces):
        offset = ((part_index - k) % count) * width
        full = lax.dynamic_update_slice_in_dim(full, piece, offset, full.ndim - 1)
    return full


def per_device(
    drafts,
    slot_of,
    lengths,
    parents,
    accepted_tokens,
    cached_key_value,
    attn_gain,
    query_weight,
    key_value_weight,
    w_out,
    mlp_gain,
    w_gate,
    w_up,
    w_down,
):
    req_count = lax.axis_size("req")
    mlp_count = lax.axis_size("mlp")
    my_index = lax.axis_index("req")
    part_index = lax.axis_index("mlp")
    per_owner_rows, tokens, quarter = drafts.shape

    rows = per_owner_rows * tokens
    w_out_all = pieces_mlp(w_out, mlp_count)
    owned_pieces = pieces_mlp(drafts.reshape(rows, quarter), mlp_count)

    local_ids = jnp.arange(per_owner_rows, dtype=jnp.int32)
    my_slots = lax.dynamic_slice_in_dim(slot_of, my_index * per_owner_rows, per_owner_rows)
    my_owners = my_slots // per_owner_rows
    owned_slots = my_index * per_owner_rows + local_ids
    requests = jnp.arange(slot_of.shape[0], dtype=jnp.int32)
    request_of = jnp.sum(
        jnp.where(slot_of[None, :] == owned_slots[:, None], requests[None, :], 0), axis=1
    )
    source_of = request_of // per_owner_rows

    outgoing = (
        jnp.zeros((req_count,) + drafts.shape[1:], drafts.dtype)
        .at[my_owners]
        .set(drafts, unique_indices=True, mode="promise_in_bounds")
    )
    incoming = lax.all_to_all(outgoing, "req", 0, 0, tiled=True)
    local_rows = jnp.take(incoming, source_of, axis=0, mode="clip")

    owner_pieces = pieces_mlp(local_rows.reshape(rows, quarter), mlp_count)
    full_rows = place_blocks(owner_pieces, mlp_count, part_index)
    wide_rows = full_rows.astype(jnp.float32)
    normalized_rows = (
        wide_rows
        * lax.rsqrt(jnp.mean(wide_rows * wide_rows, axis=1, keepdims=True) + EPS)
        * attn_gain
    ).astype(jnp.bfloat16)
    kv_heads = key_value_weight.shape[1] // (2 * HEAD_DIM)
    group_heads = query_weight.shape[1] // (kv_heads * HEAD_DIM)
    query_rows = jnp.dot(normalized_rows, query_weight, preferred_element_type=jnp.float32).reshape(
        per_owner_rows, tokens, kv_heads, group_heads, HEAD_DIM
    )
    new_key_value = (
        jnp.dot(normalized_rows, key_value_weight, preferred_element_type=jnp.float32)
        .astype(jnp.bfloat16)
        .reshape(per_owner_rows, tokens, kv_heads, 2 * HEAD_DIM)
    )
    picker = (
        accepted_tokens[:, :, None] == jnp.arange(tokens, dtype=jnp.int32)[None, None, :]
    ).astype(jnp.bfloat16)
    accepted_rows = jnp.einsum(
        "rat,rtkd->rakd", picker, new_key_value, preferred_element_type=jnp.float32
    ).astype(jnp.bfloat16)

    score_scale = 1.0 / math.sqrt(HEAD_DIM)
    draft_keys = new_key_value[..., :HEAD_DIM].astype(jnp.float32)
    draft_scores = (
        jnp.einsum("rtkgd,rjkd->rkgtj", query_rows, draft_keys, precision=HIGH) * score_scale
    )
    draft_scores = jnp.where(ancestry(parents, tokens)[:, None, None], draft_scores, -jnp.inf)
    draft_top = jnp.max(draft_scores, axis=-1)
    cache_keys = cached_key_value[..., :HEAD_DIM].astype(jnp.float32)
    scores = (
        jnp.einsum("rtkgd,rckd->rkgtc", query_rows, cache_keys, precision=HIGH) * score_scale
    )
    live_rows = jnp.arange(cached_key_value.shape[1])[None, :] < lengths[:, None]
    scores = jnp.where(live_rows[:, None, None, None, :], scores, -jnp.inf)
    row_top = jnp.maximum(draft_top, jnp.max(scores, axis=-1))
    weights = jnp.exp(scores - row_top[..., None]).astype(jnp.bfloat16)
    numerator = jnp.einsum(
        "rkgtc,rckd->rtkgd",
        weights,
        cached_key_value[..., HEAD_DIM:],
        preferred_element_type=jnp.float32,
    )
    denominator = jnp.sum(weights.astype(jnp.float32), axis=-1)
    draft_weights = jnp.exp(draft_scores - row_top[..., None]).astype(jnp.bfloat16)
    numerator = numerator + jnp.einsum(
        "rkgtj,rjkd->rtkgd",
        draft_weights,
        new_key_value[..., HEAD_DIM:],
        preferred_element_type=jnp.float32,
    )
    denominator = denominator + jnp.sum(draft_weights.astype(jnp.float32), axis=-1)
    attended = (numerator / jnp.transpose(denominator, (0, 3, 1, 2))[..., None]).astype(
        jnp.bfloat16
    )
    head_width = kv_heads * group_heads * HEAD_DIM
    attended = attended.reshape(per_owner_rows, tokens, head_width)

    returning = (
        jnp.zeros((req_count,) + attended.shape[1:], attended.dtype)
        .at[source_of]
        .set(attended, unique_indices=True, mode="promise_in_bounds")
    )
    arrived = lax.all_to_all(returning, "req", 0, 0, tiled=True)
    back_rows = jnp.take(arrived, my_owners, axis=0, mode="clip")

    gathered = pieces_mlp(back_rows.reshape(rows, head_width), mlp_count)
    owned_all = place_blocks(owned_pieces, mlp_count, part_index)

    residual = owned_all.astype(jnp.float32)
    for piece, rows_of_group in zip(gathered, w_out_all):
        group_product = jnp.dot(
            piece, rows_of_group, preferred_element_type=jnp.float32
        )
        residual = residual + group_product.astype(jnp.bfloat16).astype(jnp.float32)
    normed_two = (
        residual * lax.rsqrt(jnp.mean(residual * residual, axis=1, keepdims=True) + EPS) * mlp_gain
    ).astype(jnp.bfloat16)
    gate_out = jnp.dot(normed_two, w_gate, preferred_element_type=jnp.float32)
    up_out = jnp.dot(normed_two, w_up, preferred_element_type=jnp.float32)
    hidden = (jax.nn.silu(gate_out) * up_out).astype(jnp.bfloat16)
    unit_part = jnp.einsum(
        "tu,ujd->jtd",
        hidden,
        w_down.reshape(w_down.shape[0], mlp_count, quarter),
        preferred_element_type=jnp.float32,
    ).astype(jnp.bfloat16)

    unit_share = lax.dynamic_index_in_dim(unit_part, part_index, 0, keepdims=False).astype(
        jnp.float32
    )
    for k in range(1, mlp_count):
        target = (part_index + k) % mlp_count
        piece = lax.dynamic_index_in_dim(unit_part, target, 0, keepdims=False)
        unit_share = unit_share + shift_mlp(piece, k, mlp_count).astype(jnp.float32)
    residual_share = lax.dynamic_slice_in_dim(residual, part_index * quarter, quarter, 1)
    result = (residual_share + unit_share).astype(jnp.bfloat16)
    return (result.reshape(per_owner_rows, tokens, quarter), accepted_rows)


def solution(mesh):
    placed = (
        P("req", None, "mlp"),
        P(),
        P("req"),
        P("req", None),
        P("req", None),
        P("req", None, "mlp", None),
        P(),
        P(None, "mlp"),
        P(None, "mlp"),
        P("mlp", None),
        P(),
        P(None, "mlp"),
        P(None, "mlp"),
        P("mlp", None),
    )
    return jax.shard_map(
        per_device,
        mesh=mesh,
        in_specs=placed,
        out_specs=(P("req", None, "mlp"), P("req", None, "mlp", None)),
        check_vma=False,
    )
```

```python
import math

import jax
import jax.numpy as jnp
from jax import lax
from jax.sharding import PartitionSpec as P


HEAD_DIM = 64


EPS = 1e-06
HIGH = lax.Precision.HIGHEST


def ancestry(tree_links, tokens):
    parent_link = (
        tree_links[:, :, None] == jnp.arange(tokens, dtype=jnp.int32)[None, None, :]
    ).astype(jnp.float32)
    reachable = jnp.maximum(parent_link, jnp.eye(tokens, dtype=jnp.float32)[None])
    for _ in range(max(tokens - 1, 1).bit_length()):
        reachable = jnp.minimum(
            jnp.einsum("rij,rjk->rik", reachable, reachable, precision=HIGH), 1.0
        )
    return reachable > 0.5


def shift_mlp(value, shift, count):
    return lax.ppermute(value, "mlp", [(i, (i + shift) % count) for i in range(count)])


def pieces_mlp(value, count):
    return [value] + [shift_mlp(value, k, count) for k in range(1, count)]


def place_blocks(pieces, count, part_index):
    width = pieces[0].shape[-1]
    full = jnp.zeros(pieces[0].shape[:-1] + (width * count,), pieces[0].dtype)
    for k, piece in enumerate(pieces):
        offset = ((part_index - k) % count) * width
        full = lax.dynamic_update_slice_in_dim(full, piece, offset, full.ndim - 1)
    return full


def per_device(
    drafts,
    slot_of,
    lengths,
    parents,
    accepted_tokens,
    cached_key_value,
    attn_gain,
    query_weight,
    key_value_weight,
    w_out,
    mlp_gain,
    w_gate,
    w_up,
    w_down,
):
    req_count = lax.axis_size("req")
    mlp_count = lax.axis_size("mlp")
    my_index = lax.axis_index("req")
    part_index = lax.axis_index("mlp")
    per_owner_rows, tokens, quarter = drafts.shape

    w_out_all = pieces_mlp(w_out, mlp_count)

    local_ids = jnp.arange(per_owner_rows, dtype=jnp.int32)
    devices = jnp.arange(req_count, dtype=jnp.int32)
    my_slots = lax.dynamic_slice_in_dim(slot_of, my_index * per_owner_rows, per_owner_rows)
    my_owners = my_slots // per_owner_rows
    send_pick = jnp.sum(
        jnp.where(my_owners[None, :] == devices[:, None], local_ids[None, :], 0), axis=1
    )
    owned_slots = my_index * per_owner_rows + local_ids
    requests = jnp.arange(slot_of.shape[0], dtype=jnp.int32)
    request_of = jnp.sum(
        jnp.where(slot_of[None, :] == owned_slots[:, None], requests[None, :], 0), axis=1
    )
    source_of = request_of // per_owner_rows
    return_pick = jnp.sum(
        jnp.where(source_of[None, :] == devices[:, None], local_ids[None, :], 0), axis=1
    )

    outgoing = jnp.take(drafts, send_pick, axis=0, mode="clip")
    incoming = lax.all_to_all(outgoing, "req", 0, 0, tiled=True)
    local_rows = jnp.take(incoming, source_of, axis=0, mode="clip")

    rows = per_owner_rows * tokens
    owner_pieces = pieces_mlp(local_rows.reshape(rows, quarter), mlp_count)
    full_rows = place_blocks(owner_pieces, mlp_count, part_index)
    wide_rows = full_rows.astype(jnp.float32)
    normalized_rows = (
        wide_rows
        * lax.rsqrt(jnp.mean(wide_rows * wide_rows, axis=1, keepdims=True) + EPS)
        * attn_gain
    ).astype(jnp.bfloat16)
    kv_heads = key_value_weight.shape[1] // (2 * HEAD_DIM)
    group_heads = query_weight.shape[1] // (kv_heads * HEAD_DIM)
    query_rows = jnp.dot(normalized_rows, query_weight, preferred_element_type=jnp.float32).reshape(
        per_owner_rows, tokens, kv_heads, group_heads, HEAD_DIM
    )
    new_key_value = (
        jnp.dot(normalized_rows, key_value_weight, preferred_element_type=jnp.float32)
        .astype(jnp.bfloat16)
        .reshape(per_owner_rows, tokens, kv_heads, 2 * HEAD_DIM)
    )
    picker = (
        accepted_tokens[:, :, None] == jnp.arange(tokens, dtype=jnp.int32)[None, None, :]
    ).astype(jnp.bfloat16)
    accepted_rows = jnp.einsum(
        "rat,rtkd->rakd", picker, new_key_value, preferred_element_type=jnp.float32
    ).astype(jnp.bfloat16)

    score_scale = 1.0 / math.sqrt(HEAD_DIM)
    draft_keys = new_key_value[..., :HEAD_DIM].astype(jnp.float32)
    draft_scores = (
        jnp.einsum("rtkgd,rjkd->rkgtj", query_rows, draft_keys, precision=HIGH) * score_scale
    )
    draft_scores = jnp.where(ancestry(parents, tokens)[:, None, None], draft_scores, -jnp.inf)
    draft_top = jnp.max(draft_scores, axis=-1)
    cache_keys = cached_key_value[..., :HEAD_DIM].astype(jnp.float32)
    scores = (
        jnp.einsum("rtkgd,rckd->rkgtc", query_rows, cache_keys, precision=HIGH) * score_scale
    )
    live_rows = jnp.arange(cached_key_value.shape[1])[None, :] < lengths[:, None]
    scores = jnp.where(live_rows[:, None, None, None, :], scores, -jnp.inf)
    row_top = jnp.maximum(draft_top, jnp.max(scores, axis=-1))
    weights = jnp.exp(scores - row_top[..., None]).astype(jnp.bfloat16)
    numerator = jnp.einsum(
        "rkgtc,rckd->rtkgd",
        weights,
        cached_key_value[..., HEAD_DIM:],
        preferred_element_type=jnp.float32,
    )
    denominator = jnp.sum(weights.astype(jnp.float32), axis=-1)
    draft_weights = jnp.exp(draft_scores - row_top[..., None]).astype(jnp.bfloat16)
    numerator = numerator + jnp.einsum(
        "rkgtj,rjkd->rtkgd",
        draft_weights,
        new_key_value[..., HEAD_DIM:],
        preferred_element_type=jnp.float32,
    )
    denominator = denominator + jnp.sum(draft_weights.astype(jnp.float32), axis=-1)
    attended = (numerator / jnp.transpose(denominator, (0, 3, 1, 2))[..., None]).astype(
        jnp.bfloat16
    )
    head_width = kv_heads * group_heads * HEAD_DIM
    attended = attended.reshape(per_owner_rows, tokens, head_width)

    returning = jnp.take(attended, return_pick, axis=0, mode="clip")
    arrived = lax.all_to_all(returning, "req", 0, 0, tiled=True)
    back_rows = jnp.take(arrived, my_owners, axis=0, mode="clip")

    packed = jnp.concatenate(
        [drafts.reshape(rows, quarter), back_rows.reshape(rows, head_width)], axis=1
    )
    gathered = pieces_mlp(packed, mlp_count)
    owned_all = place_blocks([piece[:, :quarter] for piece in gathered], mlp_count, part_index)

    residual = owned_all.astype(jnp.float32)
    for piece, rows_of_group in zip(gathered, w_out_all):
        group_product = jnp.dot(
            piece[:, quarter:], rows_of_group, preferred_element_type=jnp.float32
        )
        residual = residual + group_product.astype(jnp.bfloat16).astype(jnp.float32)
    normed_two = (
        residual * lax.rsqrt(jnp.mean(residual * residual, axis=1, keepdims=True) + EPS) * mlp_gain
    ).astype(jnp.bfloat16)
    gate_out = jnp.dot(normed_two, w_gate, preferred_element_type=jnp.float32)
    up_out = jnp.dot(normed_two, w_up, preferred_element_type=jnp.float32)
    hidden = (jax.nn.silu(gate_out) * up_out).astype(jnp.bfloat16)
    def unit_block(target):
        columns = lax.dynamic_slice_in_dim(w_down, target * quarter, quarter, 1)
        return jnp.dot(hidden, columns, preferred_element_type=jnp.float32).astype(jnp.bfloat16)

    arrived_parts = []
    for k in range(1, mlp_count):
        target = (part_index + k) % mlp_count
        arrived_parts.append(shift_mlp(unit_block(target), k, mlp_count))
    unit_share = unit_block(part_index).astype(jnp.float32)
    for part in arrived_parts:
        unit_share = unit_share + part.astype(jnp.float32)
    residual_share = lax.dynamic_slice_in_dim(residual, part_index * quarter, quarter, 1)
    result = (residual_share + unit_share).astype(jnp.bfloat16)
    return (result.reshape(per_owner_rows, tokens, quarter), accepted_rows)


def solution(mesh):
    placed = (
        P("req", None, "mlp"),
        P(),
        P("req"),
        P("req", None),
        P("req", None),
        P("req", None, "mlp", None),
        P(),
        P(None, "mlp"),
        P(None, "mlp"),
        P("mlp", None),
        P(),
        P(None, "mlp"),
        P(None, "mlp"),
        P("mlp", None),
    )
    return jax.shard_map(
        per_device,
        mesh=mesh,
        in_specs=placed,
        out_specs=(P("req", None, "mlp"), P("req", None, "mlp", None)),
        check_vma=False,
    )
```

```python
import math

import jax
import jax.numpy as jnp
from jax import lax
from jax.sharding import PartitionSpec as P


HEAD_DIM = 64


EPS = 1e-06
HIGH = lax.Precision.HIGHEST


def ancestry(tree_links, tokens):
    parent_link = (
        tree_links[:, :, None] == jnp.arange(tokens, dtype=jnp.int32)[None, None, :]
    ).astype(jnp.float32)
    reachable = jnp.maximum(parent_link, jnp.eye(tokens, dtype=jnp.float32)[None])
    for _ in range(max(tokens - 1, 1).bit_length()):
        reachable = jnp.minimum(
            jnp.einsum("rij,rjk->rik", reachable, reachable, precision=HIGH), 1.0
        )
    return reachable > 0.5


def shift_mlp(value, shift, count):
    return lax.ppermute(value, "mlp", [(i, (i + shift) % count) for i in range(count)])


def pieces_mlp(value, count):
    return [value] + [shift_mlp(value, k, count) for k in range(1, count)]


def place_blocks(pieces, count, part_index):
    width = pieces[0].shape[-1]
    full = jnp.zeros(pieces[0].shape[:-1] + (width * count,), pieces[0].dtype)
    for k, piece in enumerate(pieces):
        offset = ((part_index - k) % count) * width
        full = lax.dynamic_update_slice_in_dim(full, piece, offset, full.ndim - 1)
    return full


def per_device(
    drafts,
    slot_of,
    lengths,
    parents,
    accepted_tokens,
    cached_key_value,
    attn_gain,
    query_weight,
    key_value_weight,
    w_out,
    mlp_gain,
    w_gate,
    w_up,
    w_down,
):
    req_count = lax.axis_size("req")
    mlp_count = lax.axis_size("mlp")
    my_index = lax.axis_index("req")
    part_index = lax.axis_index("mlp")
    per_owner_rows, tokens, quarter = drafts.shape

    w_out_all = pieces_mlp(w_out, mlp_count)

    local_ids = jnp.arange(per_owner_rows, dtype=jnp.int32)
    devices = jnp.arange(req_count, dtype=jnp.int32)
    my_slots = lax.dynamic_slice_in_dim(slot_of, my_index * per_owner_rows, per_owner_rows)
    my_owners = my_slots // per_owner_rows
    send_pick = jnp.sum(
        jnp.where(my_owners[None, :] == devices[:, None], local_ids[None, :], 0), axis=1
    )
    owned_slots = my_index * per_owner_rows + local_ids
    requests = jnp.arange(slot_of.shape[0], dtype=jnp.int32)
    request_of = jnp.sum(
        jnp.where(slot_of[None, :] == owned_slots[:, None], requests[None, :], 0), axis=1
    )
    source_of = request_of // per_owner_rows
    return_pick = jnp.sum(
        jnp.where(source_of[None, :] == devices[:, None], local_ids[None, :], 0), axis=1
    )

    outgoing = jnp.take(drafts, send_pick, axis=0, mode="clip")
    incoming = lax.all_to_all(outgoing, "req", 0, 0, tiled=True)
    local_rows = jnp.take(incoming, source_of, axis=0, mode="clip")

    rows = per_owner_rows * tokens
    owner_pieces = pieces_mlp(local_rows.reshape(rows, quarter), mlp_count)
    full_rows = place_blocks(owner_pieces, mlp_count, part_index)
    wide_rows = full_rows.astype(jnp.float32)
    normalized_rows = (
        wide_rows
        * lax.rsqrt(jnp.mean(wide_rows * wide_rows, axis=1, keepdims=True) + EPS)
        * attn_gain
    ).astype(jnp.bfloat16)
    kv_heads = key_value_weight.shape[1] // (2 * HEAD_DIM)
    group_heads = query_weight.shape[1] // (kv_heads * HEAD_DIM)
    query_rows = jnp.dot(normalized_rows, query_weight, preferred_element_type=jnp.float32).reshape(
        per_owner_rows, tokens, kv_heads, group_heads, HEAD_DIM
    )
    new_key_value = (
        jnp.dot(normalized_rows, key_value_weight, preferred_element_type=jnp.float32)
        .astype(jnp.bfloat16)
        .reshape(per_owner_rows, tokens, kv_heads, 2 * HEAD_DIM)
    )
    picker = (
        accepted_tokens[:, :, None] == jnp.arange(tokens, dtype=jnp.int32)[None, None, :]
    ).astype(jnp.bfloat16)
    accepted_rows = jnp.einsum(
        "rat,rtkd->rakd", picker, new_key_value, preferred_element_type=jnp.float32
    ).astype(jnp.bfloat16)

    score_scale = 1.0 / math.sqrt(HEAD_DIM)
    draft_keys = new_key_value[..., :HEAD_DIM].astype(jnp.float32)
    draft_scores = (
        jnp.einsum("rtkgd,rjkd->rkgtj", query_rows, draft_keys, precision=HIGH) * score_scale
    )
    draft_scores = jnp.where(ancestry(parents, tokens)[:, None, None], draft_scores, -jnp.inf)
    draft_top = jnp.max(draft_scores, axis=-1)
    cache_keys = cached_key_value[..., :HEAD_DIM].astype(jnp.float32)
    scores = (
        jnp.einsum("rtkgd,rckd->rkgtc", query_rows, cache_keys, precision=HIGH) * score_scale
    )
    live_rows = jnp.arange(cached_key_value.shape[1])[None, :] < lengths[:, None]
    scores = jnp.where(live_rows[:, None, None, None, :], scores, -jnp.inf)
    row_top = jnp.maximum(draft_top, jnp.max(scores, axis=-1))
    weights = jnp.exp(scores - row_top[..., None]).astype(jnp.bfloat16)
    numerator = jnp.einsum(
        "rkgtc,rckd->rtkgd",
        weights,
        cached_key_value[..., HEAD_DIM:],
        preferred_element_type=jnp.float32,
    )
    denominator = jnp.sum(weights.astype(jnp.float32), axis=-1)
    draft_weights = jnp.exp(draft_scores - row_top[..., None]).astype(jnp.bfloat16)
    numerator = numerator + jnp.einsum(
        "rkgtj,rjkd->rtkgd",
        draft_weights,
        new_key_value[..., HEAD_DIM:],
        preferred_element_type=jnp.float32,
    )
    denominator = denominator + jnp.sum(draft_weights.astype(jnp.float32), axis=-1)
    attended = (numerator / jnp.transpose(denominator, (0, 3, 1, 2))[..., None]).astype(
        jnp.bfloat16
    )
    head_width = kv_heads * group_heads * HEAD_DIM
    attended = attended.reshape(per_owner_rows, tokens, head_width)

    returning = jnp.take(attended, return_pick, axis=0, mode="clip")
    owned_pieces = pieces_mlp(drafts.reshape(rows, quarter), mlp_count)
    arrived = lax.all_to_all(returning, "req", 0, 0, tiled=True)
    back_rows = jnp.take(arrived, my_owners, axis=0, mode="clip")

    gathered = pieces_mlp(back_rows.reshape(rows, head_width), mlp_count)
    owned_all = place_blocks(owned_pieces, mlp_count, part_index)

    residual = owned_all.astype(jnp.float32)
    for piece, rows_of_group in zip(gathered, w_out_all):
        group_product = jnp.dot(
            piece, rows_of_group, preferred_element_type=jnp.float32
        )
        residual = residual + group_product.astype(jnp.bfloat16).astype(jnp.float32)
    normed_two = (
        residual * lax.rsqrt(jnp.mean(residual * residual, axis=1, keepdims=True) + EPS) * mlp_gain
    ).astype(jnp.bfloat16)
    gate_out = jnp.dot(normed_two, w_gate, preferred_element_type=jnp.float32)
    up_out = jnp.dot(normed_two, w_up, preferred_element_type=jnp.float32)
    hidden = (jax.nn.silu(gate_out) * up_out).astype(jnp.bfloat16)
    def unit_block(target):
        columns = lax.dynamic_slice_in_dim(w_down, target * quarter, quarter, 1)
        return jnp.dot(hidden, columns, preferred_element_type=jnp.float32).astype(jnp.bfloat16)

    arrived_parts = []
    for k in range(1, mlp_count):
        target = (part_index + k) % mlp_count
        arrived_parts.append(shift_mlp(unit_block(target), k, mlp_count))
    unit_share = unit_block(part_index).astype(jnp.float32)
    for part in arrived_parts:
        unit_share = unit_share + part.astype(jnp.float32)
    residual_share = lax.dynamic_slice_in_dim(residual, part_index * quarter, quarter, 1)
    result = (residual_share + unit_share).astype(jnp.bfloat16)
    return (result.reshape(per_owner_rows, tokens, quarter), accepted_rows)


def solution(mesh):
    placed = (
        P("req", None, "mlp"),
        P(),
        P("req"),
        P("req", None),
        P("req", None),
        P("req", None, "mlp", None),
        P(),
        P(None, "mlp"),
        P(None, "mlp"),
        P("mlp", None),
        P(),
        P(None, "mlp"),
        P(None, "mlp"),
        P("mlp", None),
    )
    return jax.shard_map(
        per_device,
        mesh=mesh,
        in_specs=placed,
        out_specs=(P("req", None, "mlp"), P("req", None, "mlp", None)),
        check_vma=False,
    )
```

```python
import math

import jax
import jax.numpy as jnp
from jax import lax
from jax.sharding import PartitionSpec as P


HEAD_DIM = 64


EPS = 1e-06
HIGH = lax.Precision.HIGHEST


def ancestry(tree_links, tokens):
    parent_link = (
        tree_links[:, :, None] == jnp.arange(tokens, dtype=jnp.int32)[None, None, :]
    ).astype(jnp.float32)
    reachable = jnp.maximum(parent_link, jnp.eye(tokens, dtype=jnp.float32)[None])
    for _ in range(max(tokens - 1, 1).bit_length()):
        reachable = jnp.minimum(
            jnp.einsum("rij,rjk->rik", reachable, reachable, precision=HIGH), 1.0
        )
    return reachable > 0.5


def shift_mlp(value, shift, count):
    return lax.ppermute(value, "mlp", [(i, (i + shift) % count) for i in range(count)])


def pieces_mlp(value, count):
    return [value] + [shift_mlp(value, k, count) for k in range(1, count)]


def place_blocks(pieces, count, part_index):
    width = pieces[0].shape[-1]
    full = jnp.zeros(pieces[0].shape[:-1] + (width * count,), pieces[0].dtype)
    for k, piece in enumerate(pieces):
        offset = ((part_index - k) % count) * width
        full = lax.dynamic_update_slice_in_dim(full, piece, offset, full.ndim - 1)
    return full


def per_device(
    drafts,
    slot_of,
    lengths,
    parents,
    accepted_tokens,
    cached_key_value,
    attn_gain,
    query_weight,
    key_value_weight,
    w_out,
    mlp_gain,
    w_gate,
    w_up,
    w_down,
):
    req_count = lax.axis_size("req")
    mlp_count = lax.axis_size("mlp")
    my_index = lax.axis_index("req")
    part_index = lax.axis_index("mlp")
    per_owner_rows, tokens, quarter = drafts.shape

    w_out_all = pieces_mlp(w_out, mlp_count)

    local_ids = jnp.arange(per_owner_rows, dtype=jnp.int32)
    devices = jnp.arange(req_count, dtype=jnp.int32)
    my_slots = lax.dynamic_slice_in_dim(slot_of, my_index * per_owner_rows, per_owner_rows)
    my_owners = my_slots // per_owner_rows
    send_pick = jnp.sum(
        jnp.where(my_owners[None, :] == devices[:, None], local_ids[None, :], 0), axis=1
    )
    owned_slots = my_index * per_owner_rows + local_ids
    requests = jnp.arange(slot_of.shape[0], dtype=jnp.int32)
    request_of = jnp.sum(
        jnp.where(slot_of[None, :] == owned_slots[:, None], requests[None, :], 0), axis=1
    )
    source_of = request_of // per_owner_rows
    return_pick = jnp.sum(
        jnp.where(source_of[None, :] == devices[:, None], local_ids[None, :], 0), axis=1
    )

    rows = per_owner_rows * tokens
    owned_pieces = pieces_mlp(drafts.reshape(rows, quarter), mlp_count)
    owned_all = place_blocks(owned_pieces, mlp_count, part_index)
    wide_rows = owned_all.astype(jnp.float32)
    normalized_rows = (
        wide_rows
        * lax.rsqrt(jnp.mean(wide_rows * wide_rows, axis=1, keepdims=True) + EPS)
        * attn_gain
    ).astype(jnp.bfloat16)
    kv_heads = key_value_weight.shape[1] // (2 * HEAD_DIM)
    group_heads = query_weight.shape[1] // (kv_heads * HEAD_DIM)
    query_width = kv_heads * group_heads * HEAD_DIM
    queries = jnp.dot(normalized_rows, query_weight, preferred_element_type=jnp.float32)
    fresh = jnp.dot(normalized_rows, key_value_weight, preferred_element_type=jnp.float32).astype(
        jnp.bfloat16
    )
    query_high = queries.astype(jnp.bfloat16)
    query_low = (queries - query_high.astype(jnp.float32)).astype(jnp.bfloat16)
    payload = jnp.concatenate([query_high, query_low, fresh], axis=1).reshape(
        per_owner_rows, tokens, -1
    )

    outgoing = jnp.take(payload, send_pick, axis=0, mode="clip")
    incoming = lax.all_to_all(outgoing, "req", 0, 0, tiled=True)
    local_rows = jnp.take(incoming, source_of, axis=0, mode="clip")
    query_rows = (
        local_rows[..., :query_width].astype(jnp.float32)
        + local_rows[..., query_width : 2 * query_width].astype(jnp.float32)
    ).reshape(per_owner_rows, tokens, kv_heads, group_heads, HEAD_DIM)
    new_key_value = local_rows[..., 2 * query_width :].reshape(
        per_owner_rows, tokens, kv_heads, 2 * HEAD_DIM
    )
    picker = (
        accepted_tokens[:, :, None] == jnp.arange(tokens, dtype=jnp.int32)[None, None, :]
    ).astype(jnp.bfloat16)
    accepted_rows = jnp.einsum(
        "rat,rtkd->rakd", picker, new_key_value, preferred_element_type=jnp.float32
    ).astype(jnp.bfloat16)

    score_scale = 1.0 / math.sqrt(HEAD_DIM)
    draft_keys = new_key_value[..., :HEAD_DIM].astype(jnp.float32)
    draft_scores = (
        jnp.einsum("rtkgd,rjkd->rkgtj", query_rows, draft_keys, precision=HIGH) * score_scale
    )
    draft_scores = jnp.where(ancestry(parents, tokens)[:, None, None], draft_scores, -jnp.inf)
    draft_top = jnp.max(draft_scores, axis=-1)
    cache_keys = cached_key_value[..., :HEAD_DIM].astype(jnp.float32)
    scores = (
        jnp.einsum("rtkgd,rckd->rkgtc", query_rows, cache_keys, precision=HIGH) * score_scale
    )
    live_rows = jnp.arange(cached_key_value.shape[1])[None, :] < lengths[:, None]
    scores = jnp.where(live_rows[:, None, None, None, :], scores, -jnp.inf)
    row_top = jnp.maximum(draft_top, jnp.max(scores, axis=-1))
    weights = jnp.exp(scores - row_top[..., None]).astype(jnp.bfloat16)
    numerator = jnp.einsum(
        "rkgtc,rckd->rtkgd",
        weights,
        cached_key_value[..., HEAD_DIM:],
        preferred_element_type=jnp.float32,
    )
    denominator = jnp.sum(weights.astype(jnp.float32), axis=-1)
    draft_weights = jnp.exp(draft_scores - row_top[..., None]).astype(jnp.bfloat16)
    numerator = numerator + jnp.einsum(
        "rkgtj,rjkd->rtkgd",
        draft_weights,
        new_key_value[..., HEAD_DIM:],
        preferred_element_type=jnp.float32,
    )
    denominator = denominator + jnp.sum(draft_weights.astype(jnp.float32), axis=-1)
    attended = (numerator / jnp.transpose(denominator, (0, 3, 1, 2))[..., None]).astype(
        jnp.bfloat16
    )
    head_width = kv_heads * group_heads * HEAD_DIM
    attended = attended.reshape(per_owner_rows, tokens, head_width)

    returning = jnp.take(attended, return_pick, axis=0, mode="clip")
    arrived = lax.all_to_all(returning, "req", 0, 0, tiled=True)
    back_rows = jnp.take(arrived, my_owners, axis=0, mode="clip")

    gathered = pieces_mlp(back_rows.reshape(rows, head_width), mlp_count)

    residual = owned_all.astype(jnp.float32)
    for piece, rows_of_group in zip(gathered, w_out_all):
        group_product = jnp.dot(
            piece, rows_of_group, preferred_element_type=jnp.float32
        )
        residual = residual + group_product.astype(jnp.bfloat16).astype(jnp.float32)
    normed_two = (
        residual * lax.rsqrt(jnp.mean(residual * residual, axis=1, keepdims=True) + EPS) * mlp_gain
    ).astype(jnp.bfloat16)
    gate_out = jnp.dot(normed_two, w_gate, preferred_element_type=jnp.float32)
    up_out = jnp.dot(normed_two, w_up, preferred_element_type=jnp.float32)
    hidden = (jax.nn.silu(gate_out) * up_out).astype(jnp.bfloat16)
    def unit_block(target):
        columns = lax.dynamic_slice_in_dim(w_down, target * quarter, quarter, 1)
        return jnp.dot(hidden, columns, preferred_element_type=jnp.float32).astype(jnp.bfloat16)

    arrived_parts = []
    for k in range(1, mlp_count):
        target = (part_index + k) % mlp_count
        arrived_parts.append(shift_mlp(unit_block(target), k, mlp_count))
    unit_share = unit_block(part_index).astype(jnp.float32)
    for part in arrived_parts:
        unit_share = unit_share + part.astype(jnp.float32)
    residual_share = lax.dynamic_slice_in_dim(residual, part_index * quarter, quarter, 1)
    result = (residual_share + unit_share).astype(jnp.bfloat16)
    return (result.reshape(per_owner_rows, tokens, quarter), accepted_rows)


def solution(mesh):
    placed = (
        P("req", None, "mlp"),
        P(),
        P("req"),
        P("req", None),
        P("req", None),
        P("req", None, "mlp", None),
        P(),
        P(None, "mlp"),
        P(None, "mlp"),
        P("mlp", None),
        P(),
        P(None, "mlp"),
        P(None, "mlp"),
        P("mlp", None),
    )
    return jax.shard_map(
        per_device,
        mesh=mesh,
        in_specs=placed,
        out_specs=(P("req", None, "mlp"), P("req", None, "mlp", None)),
        check_vma=False,
    )
```

```python
import math

import jax
import jax.numpy as jnp
from jax import lax
from jax.sharding import PartitionSpec as P


HEAD_DIM = 64


EPS = 1e-06
HIGH = lax.Precision.HIGHEST


def ancestry(tree_links, tokens):
    parent_link = (
        tree_links[:, :, None] == jnp.arange(tokens, dtype=jnp.int32)[None, None, :]
    ).astype(jnp.float32)
    reachable = jnp.maximum(parent_link, jnp.eye(tokens, dtype=jnp.float32)[None])
    for _ in range(max(tokens - 1, 1).bit_length()):
        reachable = jnp.minimum(
            jnp.einsum("rij,rjk->rik", reachable, reachable, precision=HIGH), 1.0
        )
    return reachable > 0.5


def shift_mlp(value, shift, count):
    return lax.ppermute(value, "mlp", [(i, (i + shift) % count) for i in range(count)])


def pieces_mlp(value, count):
    return [value] + [shift_mlp(value, k, count) for k in range(1, count)]


def place_blocks(pieces, count, part_index):
    width = pieces[0].shape[-1]
    full = jnp.zeros(pieces[0].shape[:-1] + (width * count,), pieces[0].dtype)
    for k, piece in enumerate(pieces):
        offset = ((part_index - k) % count) * width
        full = lax.dynamic_update_slice_in_dim(full, piece, offset, full.ndim - 1)
    return full


def per_device(
    drafts,
    slot_of,
    lengths,
    parents,
    accepted_tokens,
    cached_key_value,
    attn_gain,
    query_weight,
    key_value_weight,
    w_out,
    mlp_gain,
    w_gate,
    w_up,
    w_down,
):
    req_count = lax.axis_size("req")
    mlp_count = lax.axis_size("mlp")
    my_index = lax.axis_index("req")
    part_index = lax.axis_index("mlp")
    per_owner_rows, tokens, quarter = drafts.shape

    w_out_all = pieces_mlp(w_out, mlp_count)

    local_ids = jnp.arange(per_owner_rows, dtype=jnp.int32)
    devices = jnp.arange(req_count, dtype=jnp.int32)
    my_slots = lax.dynamic_slice_in_dim(slot_of, my_index * per_owner_rows, per_owner_rows)
    my_owners = my_slots // per_owner_rows
    send_pick = jnp.sum(
        jnp.where(my_owners[None, :] == devices[:, None], local_ids[None, :], 0), axis=1
    )
    owned_slots = my_index * per_owner_rows + local_ids
    requests = jnp.arange(slot_of.shape[0], dtype=jnp.int32)
    request_of = jnp.sum(
        jnp.where(slot_of[None, :] == owned_slots[:, None], requests[None, :], 0), axis=1
    )
    source_of = request_of // per_owner_rows
    return_pick = jnp.sum(
        jnp.where(source_of[None, :] == devices[:, None], local_ids[None, :], 0), axis=1
    )

    rows = per_owner_rows * tokens
    owned_pieces = pieces_mlp(drafts.reshape(rows, quarter), mlp_count)
    owned_all = place_blocks(owned_pieces, mlp_count, part_index)
    wide_rows = owned_all.astype(jnp.float32)
    normalized_rows = (
        wide_rows
        * lax.rsqrt(jnp.mean(wide_rows * wide_rows, axis=1, keepdims=True) + EPS)
        * attn_gain
    ).astype(jnp.bfloat16)
    kv_heads = key_value_weight.shape[1] // (2 * HEAD_DIM)
    group_heads = query_weight.shape[1] // (kv_heads * HEAD_DIM)
    query_width = kv_heads * group_heads * HEAD_DIM
    queries = jnp.dot(normalized_rows, query_weight, preferred_element_type=jnp.float32)
    fresh = jnp.dot(normalized_rows, key_value_weight, preferred_element_type=jnp.float32).astype(
        jnp.bfloat16
    )
    query_high = queries.astype(jnp.bfloat16)
    query_low = (queries - query_high.astype(jnp.float32)).astype(jnp.bfloat16)
    payload = jnp.concatenate([fresh, query_high, query_low], axis=1).reshape(
        per_owner_rows, tokens, -1
    )

    outgoing = jnp.take(payload, send_pick, axis=0, mode="clip")
    incoming = lax.all_to_all(outgoing, "req", 0, 0, tiled=True)
    local_rows = jnp.take(incoming, source_of, axis=0, mode="clip")
    fresh_width = fresh.shape[1]
    query_rows = (
        local_rows[..., fresh_width : fresh_width + query_width].astype(jnp.float32)
        + local_rows[..., fresh_width + query_width :].astype(jnp.float32)
    ).reshape(per_owner_rows, tokens, kv_heads, group_heads, HEAD_DIM)
    new_key_value = local_rows[..., :fresh_width].reshape(
        per_owner_rows, tokens, kv_heads, 2 * HEAD_DIM
    )
    picker = (
        accepted_tokens[:, :, None] == jnp.arange(tokens, dtype=jnp.int32)[None, None, :]
    ).astype(jnp.bfloat16)
    accepted_rows = jnp.einsum(
        "rat,rtkd->rakd", picker, new_key_value, preferred_element_type=jnp.float32
    ).astype(jnp.bfloat16)

    score_scale = 1.0 / math.sqrt(HEAD_DIM)
    draft_keys = new_key_value[..., :HEAD_DIM].astype(jnp.float32)
    draft_scores = (
        jnp.einsum("rtkgd,rjkd->rkgtj", query_rows, draft_keys, precision=HIGH) * score_scale
    )
    draft_scores = jnp.where(ancestry(parents, tokens)[:, None, None], draft_scores, -jnp.inf)
    draft_top = jnp.max(draft_scores, axis=-1)
    cache_keys = cached_key_value[..., :HEAD_DIM].astype(jnp.float32)
    scores = (
        jnp.einsum("rtkgd,rckd->rkgtc", query_rows, cache_keys, precision=HIGH) * score_scale
    )
    live_rows = jnp.arange(cached_key_value.shape[1])[None, :] < lengths[:, None]
    scores = jnp.where(live_rows[:, None, None, None, :], scores, -jnp.inf)
    row_top = jnp.maximum(draft_top, jnp.max(scores, axis=-1))
    weights = jnp.exp(scores - row_top[..., None]).astype(jnp.bfloat16)
    numerator = jnp.einsum(
        "rkgtc,rckd->rtkgd",
        weights,
        cached_key_value[..., HEAD_DIM:],
        preferred_element_type=jnp.float32,
    )
    denominator = jnp.sum(weights.astype(jnp.float32), axis=-1)
    draft_weights = jnp.exp(draft_scores - row_top[..., None]).astype(jnp.bfloat16)
    numerator = numerator + jnp.einsum(
        "rkgtj,rjkd->rtkgd",
        draft_weights,
        new_key_value[..., HEAD_DIM:],
        preferred_element_type=jnp.float32,
    )
    denominator = denominator + jnp.sum(draft_weights.astype(jnp.float32), axis=-1)
    attended = (numerator / jnp.transpose(denominator, (0, 3, 1, 2))[..., None]).astype(
        jnp.bfloat16
    )
    head_width = kv_heads * group_heads * HEAD_DIM
    attended = attended.reshape(per_owner_rows, tokens, head_width)

    returning = jnp.take(attended, return_pick, axis=0, mode="clip")
    arrived = lax.all_to_all(returning, "req", 0, 0, tiled=True)
    back_rows = jnp.take(arrived, my_owners, axis=0, mode="clip")

    gathered = pieces_mlp(back_rows.reshape(rows, head_width), mlp_count)

    group_products = [
        jnp.dot(piece, rows_of_group, preferred_element_type=jnp.float32).astype(jnp.bfloat16)
        for piece, rows_of_group in zip(gathered, w_out_all)
    ]
    attn_sum = group_products[0].astype(jnp.float32)
    for product in group_products[1:]:
        attn_sum = attn_sum + product.astype(jnp.float32)
    residual = owned_all.astype(jnp.float32) + attn_sum
    normed_two = (
        residual * lax.rsqrt(jnp.mean(residual * residual, axis=1, keepdims=True) + EPS) * mlp_gain
    ).astype(jnp.bfloat16)
    gate_out = jnp.dot(normed_two, w_gate, preferred_element_type=jnp.float32)
    up_out = jnp.dot(normed_two, w_up, preferred_element_type=jnp.float32)
    hidden = (jax.nn.silu(gate_out) * up_out).astype(jnp.bfloat16)
    def unit_block(target):
        columns = lax.dynamic_slice_in_dim(w_down, target * quarter, quarter, 1)
        return jnp.dot(hidden, columns, preferred_element_type=jnp.float32).astype(jnp.bfloat16)

    arrived_parts = []
    for k in range(1, mlp_count):
        target = (part_index + k) % mlp_count
        arrived_parts.append(shift_mlp(unit_block(target), k, mlp_count))
    unit_share = unit_block(part_index).astype(jnp.float32)
    for part in arrived_parts:
        unit_share = unit_share + part.astype(jnp.float32)
    residual_share = lax.dynamic_slice_in_dim(residual, part_index * quarter, quarter, 1)
    result = (residual_share + unit_share).astype(jnp.bfloat16)
    return (result.reshape(per_owner_rows, tokens, quarter), accepted_rows)


def solution(mesh):
    placed = (
        P("req", None, "mlp"),
        P(),
        P("req"),
        P("req", None),
        P("req", None),
        P("req", None, "mlp", None),
        P(),
        P(None, "mlp"),
        P(None, "mlp"),
        P("mlp", None),
        P(),
        P(None, "mlp"),
        P(None, "mlp"),
        P("mlp", None),
    )
    return jax.shard_map(
        per_device,
        mesh=mesh,
        in_specs=placed,
        out_specs=(P("req", None, "mlp"), P("req", None, "mlp", None)),
        check_vma=False,
    )
```

```python
import math

import jax
import jax.numpy as jnp
from jax import lax
from jax.sharding import PartitionSpec as P


HEAD_DIM = 64


EPS = 1e-06
HIGH = lax.Precision.HIGHEST


def ancestry(tree_links, tokens):
    parent_link = (
        tree_links[:, :, None] == jnp.arange(tokens, dtype=jnp.int32)[None, None, :]
    ).astype(jnp.float32)
    reachable = jnp.maximum(parent_link, jnp.eye(tokens, dtype=jnp.float32)[None])
    for _ in range(max(tokens - 1, 1).bit_length()):
        reachable = jnp.minimum(
            jnp.einsum("rij,rjk->rik", reachable, reachable, precision=HIGH), 1.0
        )
    return reachable > 0.5


def shift_mlp(value, shift, count):
    return lax.ppermute(value, "mlp", [(i, (i + shift) % count) for i in range(count)])


def pieces_mlp(value, count):
    return [value] + [shift_mlp(value, k, count) for k in range(1, count)]


def place_blocks(pieces, count, part_index):
    width = pieces[0].shape[-1]
    full = jnp.zeros(pieces[0].shape[:-1] + (width * count,), pieces[0].dtype)
    for k, piece in enumerate(pieces):
        offset = ((part_index - k) % count) * width
        full = lax.dynamic_update_slice_in_dim(full, piece, offset, full.ndim - 1)
    return full


def per_device(
    drafts,
    slot_of,
    lengths,
    parents,
    accepted_tokens,
    cached_key_value,
    attn_gain,
    query_weight,
    key_value_weight,
    w_out,
    mlp_gain,
    w_gate,
    w_up,
    w_down,
):
    req_count = lax.axis_size("req")
    mlp_count = lax.axis_size("mlp")
    my_index = lax.axis_index("req")
    part_index = lax.axis_index("mlp")
    per_owner_rows, tokens, quarter = drafts.shape

    w_out_all = pieces_mlp(w_out, mlp_count)

    local_ids = jnp.arange(per_owner_rows, dtype=jnp.int32)
    devices = jnp.arange(req_count, dtype=jnp.int32)
    my_slots = lax.dynamic_slice_in_dim(slot_of, my_index * per_owner_rows, per_owner_rows)
    my_owners = my_slots // per_owner_rows
    send_pick = jnp.sum(
        jnp.where(my_owners[None, :] == devices[:, None], local_ids[None, :], 0), axis=1
    )
    owned_slots = my_index * per_owner_rows + local_ids
    requests = jnp.arange(slot_of.shape[0], dtype=jnp.int32)
    request_of = jnp.sum(
        jnp.where(slot_of[None, :] == owned_slots[:, None], requests[None, :], 0), axis=1
    )
    source_of = request_of // per_owner_rows
    return_pick = jnp.sum(
        jnp.where(source_of[None, :] == devices[:, None], local_ids[None, :], 0), axis=1
    )

    rows = per_owner_rows * tokens
    owned_pieces = pieces_mlp(drafts.reshape(rows, quarter), mlp_count)
    owned_all = place_blocks(owned_pieces, mlp_count, part_index)
    wide_rows = owned_all.astype(jnp.float32)
    normalized_rows = (
        wide_rows
        * lax.rsqrt(jnp.mean(wide_rows * wide_rows, axis=1, keepdims=True) + EPS)
        * attn_gain
    ).astype(jnp.bfloat16)
    kv_heads = key_value_weight.shape[1] // (2 * HEAD_DIM)
    group_heads = query_weight.shape[1] // (kv_heads * HEAD_DIM)
    query_width = kv_heads * group_heads * HEAD_DIM
    queries = jnp.dot(normalized_rows, query_weight, preferred_element_type=jnp.float32)
    fresh = jnp.dot(normalized_rows, key_value_weight, preferred_element_type=jnp.float32).astype(
        jnp.bfloat16
    )
    query_high = queries.astype(jnp.bfloat16)
    query_low = (queries - query_high.astype(jnp.float32)).astype(jnp.bfloat16)
    payload = jnp.concatenate([query_high, query_low, fresh], axis=1).reshape(
        per_owner_rows, tokens, -1
    )

    outgoing = jnp.take(payload, send_pick, axis=0, mode="clip")
    incoming = lax.all_to_all(outgoing, "req", 0, 0, tiled=True)
    local_rows = jnp.take(incoming, source_of, axis=0, mode="clip")
    head_shape = (per_owner_rows, tokens, kv_heads, group_heads, HEAD_DIM)
    query_parts = (
        local_rows[..., :query_width].reshape(head_shape),
        local_rows[..., query_width : 2 * query_width].reshape(head_shape),
    )
    new_key_value = local_rows[..., 2 * query_width :].reshape(
        per_owner_rows, tokens, kv_heads, 2 * HEAD_DIM
    )
    picker = (
        accepted_tokens[:, :, None] == jnp.arange(tokens, dtype=jnp.int32)[None, None, :]
    ).astype(jnp.bfloat16)
    accepted_rows = jnp.einsum(
        "rat,rtkd->rakd", picker, new_key_value, preferred_element_type=jnp.float32
    ).astype(jnp.bfloat16)

    score_scale = 1.0 / math.sqrt(HEAD_DIM)

    def query_times(keys, spec):
        high, low = (
            jnp.einsum(spec, part, keys, preferred_element_type=jnp.float32)
            for part in query_parts
        )
        return (high + low) * score_scale

    draft_scores = query_times(new_key_value[..., :HEAD_DIM], "rtkgd,rjkd->rkgtj")
    draft_scores = jnp.where(ancestry(parents, tokens)[:, None, None], draft_scores, -jnp.inf)
    draft_top = jnp.max(draft_scores, axis=-1)
    scores = query_times(cached_key_value[..., :HEAD_DIM], "rtkgd,rckd->rkgtc")
    live_rows = jnp.arange(cached_key_value.shape[1])[None, :] < lengths[:, None]
    scores = jnp.where(live_rows[:, None, None, None, :], scores, -jnp.inf)
    row_top = jnp.maximum(draft_top, jnp.max(scores, axis=-1))
    weights = jnp.exp(scores - row_top[..., None]).astype(jnp.bfloat16)
    numerator = jnp.einsum(
        "rkgtc,rckd->rtkgd",
        weights,
        cached_key_value[..., HEAD_DIM:],
        preferred_element_type=jnp.float32,
    )
    denominator = jnp.sum(weights.astype(jnp.float32), axis=-1)
    draft_weights = jnp.exp(draft_scores - row_top[..., None]).astype(jnp.bfloat16)
    numerator = numerator + jnp.einsum(
        "rkgtj,rjkd->rtkgd",
        draft_weights,
        new_key_value[..., HEAD_DIM:],
        preferred_element_type=jnp.float32,
    )
    denominator = denominator + jnp.sum(draft_weights.astype(jnp.float32), axis=-1)
    attended = (numerator / jnp.transpose(denominator, (0, 3, 1, 2))[..., None]).astype(
        jnp.bfloat16
    )
    head_width = kv_heads * group_heads * HEAD_DIM
    attended = attended.reshape(per_owner_rows, tokens, head_width)

    returning = jnp.take(attended, return_pick, axis=0, mode="clip")
    arrived = lax.all_to_all(returning, "req", 0, 0, tiled=True)
    back_rows = jnp.take(arrived, my_owners, axis=0, mode="clip")

    gathered = pieces_mlp(back_rows.reshape(rows, head_width), mlp_count)

    residual = owned_all.astype(jnp.float32)
    for piece, rows_of_group in zip(gathered, w_out_all):
        group_product = jnp.dot(
            piece, rows_of_group, preferred_element_type=jnp.float32
        )
        residual = residual + group_product.astype(jnp.bfloat16).astype(jnp.float32)
    normed_two = (
        residual * lax.rsqrt(jnp.mean(residual * residual, axis=1, keepdims=True) + EPS) * mlp_gain
    ).astype(jnp.bfloat16)
    gate_out = jnp.dot(normed_two, w_gate, preferred_element_type=jnp.float32)
    up_out = jnp.dot(normed_two, w_up, preferred_element_type=jnp.float32)
    hidden = (jax.nn.silu(gate_out) * up_out).astype(jnp.bfloat16)

    def unit_block(target):
        columns = lax.dynamic_slice_in_dim(w_down, target * quarter, quarter, 1)
        return jnp.dot(hidden, columns, preferred_element_type=jnp.float32).astype(jnp.bfloat16)

    arrived_parts = []
    for k in range(1, mlp_count):
        target = (part_index + k) % mlp_count
        arrived_parts.append(shift_mlp(unit_block(target), k, mlp_count))
    unit_share = unit_block(part_index).astype(jnp.float32)
    for part in arrived_parts:
        unit_share = unit_share + part.astype(jnp.float32)
    residual_share = lax.dynamic_slice_in_dim(residual, part_index * quarter, quarter, 1)
    result = (residual_share + unit_share).astype(jnp.bfloat16)
    return (result.reshape(per_owner_rows, tokens, quarter), accepted_rows)


def solution(mesh):
    placed = (
        P("req", None, "mlp"),
        P(),
        P("req"),
        P("req", None),
        P("req", None),
        P("req", None, "mlp", None),
        P(),
        P(None, "mlp"),
        P(None, "mlp"),
        P("mlp", None),
        P(),
        P(None, "mlp"),
        P(None, "mlp"),
        P("mlp", None),
    )
    return jax.shard_map(
        per_device,
        mesh=mesh,
        in_specs=placed,
        out_specs=(P("req", None, "mlp"), P("req", None, "mlp", None)),
        check_vma=False,
    )
```

```python
import functools
import math

import jax
import jax.numpy as jnp
from jax import lax
from jax.sharding import PartitionSpec as P

from jax.experimental import pallas as pl
from jax.experimental.pallas import tpu as pltpu


HEAD_DIM = 64


EPS = 1e-06
HIGH = lax.Precision.HIGHEST


def ancestry(tree_links, tokens):
    parent_link = (
        tree_links[:, :, None] == jnp.arange(tokens, dtype=jnp.int32)[None, None, :]
    ).astype(jnp.float32)
    reachable = jnp.maximum(parent_link, jnp.eye(tokens, dtype=jnp.float32)[None])
    for _ in range(max(tokens - 1, 1).bit_length()):
        reachable = jnp.minimum(
            jnp.einsum("rij,rjk->rik", reachable, reachable, precision=HIGH), 1.0
        )
    return reachable > 0.5


def shift_mlp(value, shift, count):
    return lax.ppermute(value, "mlp", [(i, (i + shift) % count) for i in range(count)])


def pieces_mlp(value, count):
    return [value] + [shift_mlp(value, k, count) for k in range(1, count)]


def place_blocks(pieces, count, part_index):
    width = pieces[0].shape[-1]
    full = jnp.zeros(pieces[0].shape[:-1] + (width * count,), pieces[0].dtype)
    for k, piece in enumerate(pieces):
        offset = ((part_index - k) % count) * width
        full = lax.dynamic_update_slice_in_dim(full, piece, offset, full.ndim - 1)
    return full


def attend_kernel(source_ref, length_ref, row_ref, cache_ref, mask_ref, out_ref, *, widths):
    query_width, group_heads = widths
    slot = pl.program_id(0)
    row = row_ref[0]
    cache = cache_ref[0, :, 0, :]
    keys_cache, values_cache = cache[:, :HEAD_DIM], cache[:, HEAD_DIM:]
    fresh = row[:, 2 * query_width :]
    keys_draft, values_draft = fresh[:, :HEAD_DIM], fresh[:, HEAD_DIM:]
    live = lax.broadcasted_iota(jnp.int32, (1, cache.shape[0]), 1) < length_ref[slot]
    visible = mask_ref[0] > 0.5
    scale = 1.0 / math.sqrt(HEAD_DIM)
    contract = (((1,), (1,)), ((), ()))

    def times(part, keys):
        return lax.dot_general(part, keys, contract, preferred_element_type=jnp.float32)

    outs = []
    for g in range(group_heads):
        high = row[:, g * HEAD_DIM : (g + 1) * HEAD_DIM]
        low = row[:, query_width + g * HEAD_DIM : query_width + (g + 1) * HEAD_DIM]
        score_cache = (times(high, keys_cache) + times(low, keys_cache)) * scale
        score_cache = jnp.where(live, score_cache, -jnp.inf)
        score_draft = (times(high, keys_draft) + times(low, keys_draft)) * scale
        score_draft = jnp.where(visible, score_draft, -jnp.inf)
        top = jnp.maximum(
            jnp.max(score_cache, axis=1, keepdims=True), jnp.max(score_draft, axis=1, keepdims=True)
        )
        weight_cache = jnp.exp(score_cache - top).astype(jnp.bfloat16)
        weight_draft = jnp.exp(score_draft - top).astype(jnp.bfloat16)
        numerator = jnp.dot(
            weight_cache, values_cache, preferred_element_type=jnp.float32
        ) + jnp.dot(weight_draft, values_draft, preferred_element_type=jnp.float32)
        denominator = jnp.sum(weight_cache.astype(jnp.float32), axis=1, keepdims=True) + jnp.sum(
            weight_draft.astype(jnp.float32), axis=1, keepdims=True
        )
        outs.append((numerator / denominator).astype(jnp.bfloat16))
    out_ref[0] = jnp.concatenate(outs, axis=1)


def per_device(
    drafts,
    slot_of,
    lengths,
    parents,
    accepted_tokens,
    cached_key_value,
    attn_gain,
    query_weight,
    key_value_weight,
    w_out,
    mlp_gain,
    w_gate,
    w_up,
    w_down,
):
    req_count = lax.axis_size("req")
    mlp_count = lax.axis_size("mlp")
    my_index = lax.axis_index("req")
    part_index = lax.axis_index("mlp")
    per_owner_rows, tokens, quarter = drafts.shape

    w_out_all = pieces_mlp(w_out, mlp_count)

    local_ids = jnp.arange(per_owner_rows, dtype=jnp.int32)
    devices = jnp.arange(req_count, dtype=jnp.int32)
    my_slots = lax.dynamic_slice_in_dim(slot_of, my_index * per_owner_rows, per_owner_rows)
    my_owners = my_slots // per_owner_rows
    send_pick = jnp.sum(
        jnp.where(my_owners[None, :] == devices[:, None], local_ids[None, :], 0), axis=1
    )
    owned_slots = my_index * per_owner_rows + local_ids
    requests = jnp.arange(slot_of.shape[0], dtype=jnp.int32)
    request_of = jnp.sum(
        jnp.where(slot_of[None, :] == owned_slots[:, None], requests[None, :], 0), axis=1
    )
    source_of = request_of // per_owner_rows

    rows = per_owner_rows * tokens
    owned_pieces = pieces_mlp(drafts.reshape(rows, quarter), mlp_count)
    owned_all = place_blocks(owned_pieces, mlp_count, part_index)
    wide_rows = owned_all.astype(jnp.float32)
    normalized_rows = (
        wide_rows
        * lax.rsqrt(jnp.mean(wide_rows * wide_rows, axis=1, keepdims=True) + EPS)
        * attn_gain
    ).astype(jnp.bfloat16)
    kv_heads = key_value_weight.shape[1] // (2 * HEAD_DIM)
    group_heads = query_weight.shape[1] // (kv_heads * HEAD_DIM)
    query_width = kv_heads * group_heads * HEAD_DIM
    queries = jnp.dot(normalized_rows, query_weight, preferred_element_type=jnp.float32)
    fresh = jnp.dot(normalized_rows, key_value_weight, preferred_element_type=jnp.float32).astype(
        jnp.bfloat16
    )
    query_high = queries.astype(jnp.bfloat16)
    query_low = (queries - query_high.astype(jnp.float32)).astype(jnp.bfloat16)
    payload = jnp.concatenate([query_high, query_low, fresh], axis=1).reshape(
        per_owner_rows, tokens, -1
    )

    outgoing = jnp.take(payload, send_pick, axis=0, mode="clip")
    incoming = lax.all_to_all(outgoing, "req", 0, 0, tiled=True)
    local_rows = jnp.take(incoming, source_of, axis=0, mode="clip")
    new_key_value = local_rows[..., 2 * query_width :].reshape(
        per_owner_rows, tokens, kv_heads, 2 * HEAD_DIM
    )
    picker = (
        accepted_tokens[:, :, None] == jnp.arange(tokens, dtype=jnp.int32)[None, None, :]
    ).astype(jnp.bfloat16)
    accepted_rows = jnp.einsum(
        "rat,rtkd->rakd", picker, new_key_value, preferred_element_type=jnp.float32
    ).astype(jnp.bfloat16)

    visible = ancestry(parents, tokens).astype(jnp.float32)
    head_width = kv_heads * group_heads * HEAD_DIM
    cache_len = cached_key_value.shape[1]
    grid_spec = pltpu.PrefetchScalarGridSpec(
        num_scalar_prefetch=2,
        grid=(per_owner_rows,),
        in_specs=[
            pl.BlockSpec((1, tokens, incoming.shape[2]), lambda j, src, lens: (src[j], 0, 0)),
            pl.BlockSpec((1, cache_len, 1, 2 * HEAD_DIM), lambda j, src, lens: (j, 0, 0, 0)),
            pl.BlockSpec((1, tokens, tokens), lambda j, src, lens: (j, 0, 0)),
        ],
        out_specs=pl.BlockSpec((1, tokens, head_width), lambda j, src, lens: (src[j], 0, 0)),
    )
    returning = pl.pallas_call(
        functools.partial(attend_kernel, widths=(query_width, group_heads)),
        grid_spec=grid_spec,
        out_shape=jax.ShapeDtypeStruct((req_count, tokens, head_width), jnp.bfloat16),
    )(source_of, lengths, incoming, cached_key_value, visible)

    arrived = lax.all_to_all(returning, "req", 0, 0, tiled=True)
    back_rows = jnp.take(arrived, my_owners, axis=0, mode="clip")

    gathered = pieces_mlp(back_rows.reshape(rows, head_width), mlp_count)

    residual = owned_all.astype(jnp.float32)
    for piece, rows_of_group in zip(gathered, w_out_all):
        group_product = jnp.dot(
            piece, rows_of_group, preferred_element_type=jnp.float32
        )
        residual = residual + group_product.astype(jnp.bfloat16).astype(jnp.float32)
    normed_two = (
        residual * lax.rsqrt(jnp.mean(residual * residual, axis=1, keepdims=True) + EPS) * mlp_gain
    ).astype(jnp.bfloat16)
    gate_out = jnp.dot(normed_two, w_gate, preferred_element_type=jnp.float32)
    up_out = jnp.dot(normed_two, w_up, preferred_element_type=jnp.float32)
    hidden = (jax.nn.silu(gate_out) * up_out).astype(jnp.bfloat16)

    def unit_block(target):
        columns = lax.dynamic_slice_in_dim(w_down, target * quarter, quarter, 1)
        return jnp.dot(hidden, columns, preferred_element_type=jnp.float32).astype(jnp.bfloat16)

    arrived_parts = []
    for k in range(1, mlp_count):
        target = (part_index + k) % mlp_count
        arrived_parts.append(shift_mlp(unit_block(target), k, mlp_count))
    unit_share = unit_block(part_index).astype(jnp.float32)
    for part in arrived_parts:
        unit_share = unit_share + part.astype(jnp.float32)
    residual_share = lax.dynamic_slice_in_dim(residual, part_index * quarter, quarter, 1)
    result = (residual_share + unit_share).astype(jnp.bfloat16)
    return (result.reshape(per_owner_rows, tokens, quarter), accepted_rows)


def solution(mesh):
    placed = (
        P("req", None, "mlp"),
        P(),
        P("req"),
        P("req", None),
        P("req", None),
        P("req", None, "mlp", None),
        P(),
        P(None, "mlp"),
        P(None, "mlp"),
        P("mlp", None),
        P(),
        P(None, "mlp"),
        P(None, "mlp"),
        P("mlp", None),
    )
    return jax.shard_map(
        per_device,
        mesh=mesh,
        in_specs=placed,
        out_specs=(P("req", None, "mlp"), P("req", None, "mlp", None)),
        check_vma=False,
    )
```

```python
import functools
import math

import jax
import jax.numpy as jnp
from jax import lax
from jax.sharding import PartitionSpec as P

from jax.experimental import pallas as pl
from jax.experimental.pallas import tpu as pltpu


HEAD_DIM = 64


EPS = 1e-06
HIGH = lax.Precision.HIGHEST


def ancestry(tree_links, tokens):
    parent_link = (
        tree_links[:, :, None] == jnp.arange(tokens, dtype=jnp.int32)[None, None, :]
    ).astype(jnp.float32)
    reachable = jnp.maximum(parent_link, jnp.eye(tokens, dtype=jnp.float32)[None])
    for _ in range(max(tokens - 1, 1).bit_length()):
        reachable = jnp.minimum(
            jnp.einsum("rij,rjk->rik", reachable, reachable, precision=HIGH), 1.0
        )
    return reachable > 0.5


def shift_mlp(value, shift, count):
    return lax.ppermute(value, "mlp", [(i, (i + shift) % count) for i in range(count)])


def pieces_mlp(value, count):
    return [value] + [shift_mlp(value, k, count) for k in range(1, count)]


def place_blocks(pieces, count, part_index):
    width = pieces[0].shape[-1]
    full = jnp.zeros(pieces[0].shape[:-1] + (width * count,), pieces[0].dtype)
    for k, piece in enumerate(pieces):
        offset = ((part_index - k) % count) * width
        full = lax.dynamic_update_slice_in_dim(full, piece, offset, full.ndim - 1)
    return full


def attend_kernel(source_ref, length_ref, row_ref, cache_ref, mask_ref, out_ref, *, widths):
    query_width, group_heads = widths
    slot = pl.program_id(0)
    row = row_ref[0]
    cache = cache_ref[0]
    keys_cache, values_cache = cache[:, :HEAD_DIM], cache[:, HEAD_DIM:]
    fresh = row[:, 2 * query_width :]
    keys_draft, values_draft = fresh[:, :HEAD_DIM], fresh[:, HEAD_DIM:]
    live = lax.broadcasted_iota(jnp.int32, (1, cache.shape[0]), 1) < length_ref[slot]
    visible = mask_ref[0] > 0.5
    scale = 1.0 / math.sqrt(HEAD_DIM)
    contract = (((1,), (1,)), ((), ()))

    def times(part, keys):
        return lax.dot_general(part, keys, contract, preferred_element_type=jnp.float32)

    outs = []
    for g in range(group_heads):
        high = row[:, g * HEAD_DIM : (g + 1) * HEAD_DIM]
        low = row[:, query_width + g * HEAD_DIM : query_width + (g + 1) * HEAD_DIM]
        score_cache = (times(high, keys_cache) + times(low, keys_cache)) * scale
        score_cache = jnp.where(live, score_cache, -jnp.inf)
        score_draft = (times(high, keys_draft) + times(low, keys_draft)) * scale
        score_draft = jnp.where(visible, score_draft, -jnp.inf)
        top = jnp.maximum(
            jnp.max(score_cache, axis=1, keepdims=True), jnp.max(score_draft, axis=1, keepdims=True)
        )
        weight_cache = jnp.exp(score_cache - top).astype(jnp.bfloat16)
        weight_draft = jnp.exp(score_draft - top).astype(jnp.bfloat16)
        numerator = jnp.dot(
            weight_cache, values_cache, preferred_element_type=jnp.float32
        ) + jnp.dot(weight_draft, values_draft, preferred_element_type=jnp.float32)
        denominator = jnp.sum(weight_cache.astype(jnp.float32), axis=1, keepdims=True) + jnp.sum(
            weight_draft.astype(jnp.float32), axis=1, keepdims=True
        )
        outs.append((numerator / denominator).astype(jnp.bfloat16))
    out_ref[0] = jnp.concatenate(outs, axis=1)


def per_device(
    drafts,
    slot_of,
    lengths,
    parents,
    accepted_tokens,
    cached_key_value,
    attn_gain,
    query_weight,
    key_value_weight,
    w_out,
    mlp_gain,
    w_gate,
    w_up,
    w_down,
):
    req_count = lax.axis_size("req")
    mlp_count = lax.axis_size("mlp")
    my_index = lax.axis_index("req")
    part_index = lax.axis_index("mlp")
    per_owner_rows, tokens, quarter = drafts.shape

    w_out_all = pieces_mlp(w_out, mlp_count)

    local_ids = jnp.arange(per_owner_rows, dtype=jnp.int32)
    devices = jnp.arange(req_count, dtype=jnp.int32)
    my_slots = lax.dynamic_slice_in_dim(slot_of, my_index * per_owner_rows, per_owner_rows)
    my_owners = my_slots // per_owner_rows
    send_pick = jnp.sum(
        jnp.where(my_owners[None, :] == devices[:, None], local_ids[None, :], 0), axis=1
    )
    owned_slots = my_index * per_owner_rows + local_ids
    requests = jnp.arange(slot_of.shape[0], dtype=jnp.int32)
    request_of = jnp.sum(
        jnp.where(slot_of[None, :] == owned_slots[:, None], requests[None, :], 0), axis=1
    )
    source_of = request_of // per_owner_rows

    rows = per_owner_rows * tokens
    owned_pieces = pieces_mlp(drafts.reshape(rows, quarter), mlp_count)
    owned_all = place_blocks(owned_pieces, mlp_count, part_index)
    wide_rows = owned_all.astype(jnp.float32)
    normalized_rows = (
        wide_rows
        * lax.rsqrt(jnp.mean(wide_rows * wide_rows, axis=1, keepdims=True) + EPS)
        * attn_gain
    ).astype(jnp.bfloat16)
    kv_heads = key_value_weight.shape[1] // (2 * HEAD_DIM)
    group_heads = query_weight.shape[1] // (kv_heads * HEAD_DIM)
    query_width = kv_heads * group_heads * HEAD_DIM
    queries = jnp.dot(normalized_rows, query_weight, preferred_element_type=jnp.float32)
    fresh = jnp.dot(normalized_rows, key_value_weight, preferred_element_type=jnp.float32).astype(
        jnp.bfloat16
    )
    query_high = queries.astype(jnp.bfloat16)
    query_low = (queries - query_high.astype(jnp.float32)).astype(jnp.bfloat16)
    payload = jnp.concatenate([query_high, query_low, fresh], axis=1).reshape(
        per_owner_rows, tokens, -1
    )

    outgoing = jnp.take(payload, send_pick, axis=0, mode="clip")
    incoming = lax.all_to_all(outgoing, "req", 0, 0, tiled=True)
    local_rows = jnp.take(incoming, source_of, axis=0, mode="clip")
    new_key_value = local_rows[..., 2 * query_width :].reshape(
        per_owner_rows, tokens, kv_heads, 2 * HEAD_DIM
    )
    picker = (
        accepted_tokens[:, :, None] == jnp.arange(tokens, dtype=jnp.int32)[None, None, :]
    ).astype(jnp.bfloat16)
    accepted_rows = jnp.einsum(
        "rat,rtkd->rakd", picker, new_key_value, preferred_element_type=jnp.float32
    ).astype(jnp.bfloat16)

    visible = ancestry(parents, tokens).astype(jnp.float32)
    head_width = kv_heads * group_heads * HEAD_DIM
    cache_len = cached_key_value.shape[1]
    grid_spec = pltpu.PrefetchScalarGridSpec(
        num_scalar_prefetch=2,
        grid=(per_owner_rows,),
        in_specs=[
            pl.BlockSpec((1, tokens, incoming.shape[2]), lambda j, src, lens: (src[j], 0, 0)),
            pl.BlockSpec((1, cache_len, 2 * HEAD_DIM), lambda j, src, lens: (j, 0, 0)),
            pl.BlockSpec((1, tokens, tokens), lambda j, src, lens: (j, 0, 0)),
        ],
        out_specs=pl.BlockSpec((1, tokens, head_width), lambda j, src, lens: (src[j], 0, 0)),
    )
    returning = pl.pallas_call(
        functools.partial(attend_kernel, widths=(query_width, group_heads)),
        grid_spec=grid_spec,
        out_shape=jax.ShapeDtypeStruct((req_count, tokens, head_width), jnp.bfloat16),
    )(
        source_of,
        lengths,
        incoming,
        cached_key_value.reshape(per_owner_rows, cache_len, 2 * HEAD_DIM),
        visible,
    )

    arrived = lax.all_to_all(returning, "req", 0, 0, tiled=True)
    back_rows = jnp.take(arrived, my_owners, axis=0, mode="clip")

    gathered = pieces_mlp(back_rows.reshape(rows, head_width), mlp_count)

    residual = owned_all.astype(jnp.float32)
    for piece, rows_of_group in zip(gathered, w_out_all):
        group_product = jnp.dot(
            piece, rows_of_group, preferred_element_type=jnp.float32
        )
        residual = residual + group_product.astype(jnp.bfloat16).astype(jnp.float32)
    normed_two = (
        residual * lax.rsqrt(jnp.mean(residual * residual, axis=1, keepdims=True) + EPS) * mlp_gain
    ).astype(jnp.bfloat16)
    gate_out = jnp.dot(normed_two, w_gate, preferred_element_type=jnp.float32)
    up_out = jnp.dot(normed_two, w_up, preferred_element_type=jnp.float32)
    hidden = (jax.nn.silu(gate_out) * up_out).astype(jnp.bfloat16)

    def unit_block(target):
        columns = lax.dynamic_slice_in_dim(w_down, target * quarter, quarter, 1)
        return jnp.dot(hidden, columns, preferred_element_type=jnp.float32).astype(jnp.bfloat16)

    arrived_parts = []
    for k in range(1, mlp_count):
        target = (part_index + k) % mlp_count
        arrived_parts.append(shift_mlp(unit_block(target), k, mlp_count))
    unit_share = unit_block(part_index).astype(jnp.float32)
    for part in arrived_parts:
        unit_share = unit_share + part.astype(jnp.float32)
    residual_share = lax.dynamic_slice_in_dim(residual, part_index * quarter, quarter, 1)
    result = (residual_share + unit_share).astype(jnp.bfloat16)
    return (result.reshape(per_owner_rows, tokens, quarter), accepted_rows)


def solution(mesh):
    placed = (
        P("req", None, "mlp"),
        P(),
        P("req"),
        P("req", None),
        P("req", None),
        P("req", None, "mlp", None),
        P(),
        P(None, "mlp"),
        P(None, "mlp"),
        P("mlp", None),
        P(),
        P(None, "mlp"),
        P(None, "mlp"),
        P("mlp", None),
    )
    return jax.shard_map(
        per_device,
        mesh=mesh,
        in_specs=placed,
        out_specs=(P("req", None, "mlp"), P("req", None, "mlp", None)),
        check_vma=False,
    )
```

```python
import functools
import math

import jax
import jax.numpy as jnp
from jax import lax
from jax.sharding import PartitionSpec as P

from jax.experimental import pallas as pl
from jax.experimental.pallas import tpu as pltpu


HEAD_DIM = 64


EPS = 1e-06
HIGH = lax.Precision.HIGHEST


def ancestry(tree_links, tokens):
    parent_link = (
        tree_links[:, :, None] == jnp.arange(tokens, dtype=jnp.int32)[None, None, :]
    ).astype(jnp.float32)
    reachable = jnp.maximum(parent_link, jnp.eye(tokens, dtype=jnp.float32)[None])
    for _ in range(max(tokens - 1, 1).bit_length()):
        reachable = jnp.minimum(
            jnp.einsum("rij,rjk->rik", reachable, reachable, precision=HIGH), 1.0
        )
    return reachable > 0.5


def shift_mlp(value, shift, count):
    return lax.ppermute(value, "mlp", [(i, (i + shift) % count) for i in range(count)])


def pieces_mlp(value, count):
    return [value] + [shift_mlp(value, k, count) for k in range(1, count)]


def place_blocks(pieces, count, part_index):
    width = pieces[0].shape[-1]
    full = jnp.zeros(pieces[0].shape[:-1] + (width * count,), pieces[0].dtype)
    for k, piece in enumerate(pieces):
        offset = ((part_index - k) % count) * width
        full = lax.dynamic_update_slice_in_dim(full, piece, offset, full.ndim - 1)
    return full


def attend_kernel(source_ref, length_ref, row_ref, cache_ref, mask_ref, out_ref, *, widths):
    query_width, group_heads = widths
    slot = pl.program_id(0)
    row = row_ref[0]
    tokens = row.shape[0]
    cache = cache_ref[0]
    keys_cache = cache[:, :HEAD_DIM].T
    values_cache = cache[:, HEAD_DIM:]
    fresh = row[:, 2 * query_width :]
    keys_draft = fresh[:, :HEAD_DIM].T
    values_draft = fresh[:, HEAD_DIM:]
    live = lax.broadcasted_iota(jnp.int32, (1, cache.shape[0]), 1) < length_ref[slot]
    visible = jnp.concatenate([mask_ref[0]] * group_heads, axis=0) > 0.5
    scale = 1.0 / math.sqrt(HEAD_DIM)

    def stacked(offset):
        return jnp.concatenate(
            [row[:, offset + g * HEAD_DIM : offset + (g + 1) * HEAD_DIM] for g in range(group_heads)],
            axis=0,
        )

    high, low = stacked(0), stacked(query_width)

    def times(keys):
        return (
            jnp.dot(high, keys, preferred_element_type=jnp.float32)
            + jnp.dot(low, keys, preferred_element_type=jnp.float32)
        ) * scale

    score_cache = jnp.where(live, times(keys_cache), -jnp.inf)
    score_draft = jnp.where(visible, times(keys_draft), -jnp.inf)
    top = jnp.maximum(
        jnp.max(score_cache, axis=1, keepdims=True), jnp.max(score_draft, axis=1, keepdims=True)
    )
    weight_cache = jnp.exp(score_cache - top).astype(jnp.bfloat16)
    weight_draft = jnp.exp(score_draft - top).astype(jnp.bfloat16)
    numerator = jnp.dot(weight_cache, values_cache, preferred_element_type=jnp.float32) + jnp.dot(
        weight_draft, values_draft, preferred_element_type=jnp.float32
    )
    denominator = jnp.sum(weight_cache.astype(jnp.float32), axis=1, keepdims=True) + jnp.sum(
        weight_draft.astype(jnp.float32), axis=1, keepdims=True
    )
    attended = (numerator / denominator).astype(jnp.bfloat16)
    out_ref[0] = jnp.concatenate(
        [attended[g * tokens : (g + 1) * tokens] for g in range(group_heads)], axis=1
    )


def per_device(
    drafts,
    slot_of,
    lengths,
    parents,
    accepted_tokens,
    cached_key_value,
    attn_gain,
    query_weight,
    key_value_weight,
    w_out,
    mlp_gain,
    w_gate,
    w_up,
    w_down,
):
    req_count = lax.axis_size("req")
    mlp_count = lax.axis_size("mlp")
    my_index = lax.axis_index("req")
    part_index = lax.axis_index("mlp")
    per_owner_rows, tokens, quarter = drafts.shape

    w_out_all = pieces_mlp(w_out, mlp_count)

    local_ids = jnp.arange(per_owner_rows, dtype=jnp.int32)
    devices = jnp.arange(req_count, dtype=jnp.int32)
    my_slots = lax.dynamic_slice_in_dim(slot_of, my_index * per_owner_rows, per_owner_rows)
    my_owners = my_slots // per_owner_rows
    send_pick = jnp.sum(
        jnp.where(my_owners[None, :] == devices[:, None], local_ids[None, :], 0), axis=1
    )
    owned_slots = my_index * per_owner_rows + local_ids
    requests = jnp.arange(slot_of.shape[0], dtype=jnp.int32)
    request_of = jnp.sum(
        jnp.where(slot_of[None, :] == owned_slots[:, None], requests[None, :], 0), axis=1
    )
    source_of = request_of // per_owner_rows

    rows = per_owner_rows * tokens
    owned_pieces = pieces_mlp(drafts.reshape(rows, quarter), mlp_count)
    owned_all = place_blocks(owned_pieces, mlp_count, part_index)
    wide_rows = owned_all.astype(jnp.float32)
    normalized_rows = (
        wide_rows
        * lax.rsqrt(jnp.mean(wide_rows * wide_rows, axis=1, keepdims=True) + EPS)
        * attn_gain
    ).astype(jnp.bfloat16)
    kv_heads = key_value_weight.shape[1] // (2 * HEAD_DIM)
    group_heads = query_weight.shape[1] // (kv_heads * HEAD_DIM)
    query_width = kv_heads * group_heads * HEAD_DIM
    queries = jnp.dot(normalized_rows, query_weight, preferred_element_type=jnp.float32)
    fresh = jnp.dot(normalized_rows, key_value_weight, preferred_element_type=jnp.float32).astype(
        jnp.bfloat16
    )
    query_high = queries.astype(jnp.bfloat16)
    query_low = (queries - query_high.astype(jnp.float32)).astype(jnp.bfloat16)
    payload = jnp.concatenate([query_high, query_low, fresh], axis=1).reshape(
        per_owner_rows, tokens, -1
    )

    outgoing = jnp.take(payload, send_pick, axis=0, mode="clip")
    incoming = lax.all_to_all(outgoing, "req", 0, 0, tiled=True)
    local_rows = jnp.take(incoming, source_of, axis=0, mode="clip")
    new_key_value = local_rows[..., 2 * query_width :].reshape(
        per_owner_rows, tokens, kv_heads, 2 * HEAD_DIM
    )
    picker = (
        accepted_tokens[:, :, None] == jnp.arange(tokens, dtype=jnp.int32)[None, None, :]
    ).astype(jnp.bfloat16)
    accepted_rows = jnp.einsum(
        "rat,rtkd->rakd", picker, new_key_value, preferred_element_type=jnp.float32
    ).astype(jnp.bfloat16)

    visible = ancestry(parents, tokens).astype(jnp.float32)
    head_width = kv_heads * group_heads * HEAD_DIM
    cache_len = cached_key_value.shape[1]
    grid_spec = pltpu.PrefetchScalarGridSpec(
        num_scalar_prefetch=2,
        grid=(per_owner_rows,),
        in_specs=[
            pl.BlockSpec((1, tokens, incoming.shape[2]), lambda j, src, lens: (src[j], 0, 0)),
            pl.BlockSpec((1, cache_len, 2 * HEAD_DIM), lambda j, src, lens: (j, 0, 0)),
            pl.BlockSpec((1, tokens, tokens), lambda j, src, lens: (j, 0, 0)),
        ],
        out_specs=pl.BlockSpec((1, tokens, head_width), lambda j, src, lens: (src[j], 0, 0)),
    )
    returning = pl.pallas_call(
        functools.partial(attend_kernel, widths=(query_width, group_heads)),
        grid_spec=grid_spec,
        out_shape=jax.ShapeDtypeStruct((req_count, tokens, head_width), jnp.bfloat16),
    )(
        source_of,
        lengths,
        incoming,
        cached_key_value.reshape(per_owner_rows, cache_len, 2 * HEAD_DIM),
        visible,
    )

    arrived = lax.all_to_all(returning, "req", 0, 0, tiled=True)
    back_rows = jnp.take(arrived, my_owners, axis=0, mode="clip")

    gathered = pieces_mlp(back_rows.reshape(rows, head_width), mlp_count)

    residual = owned_all.astype(jnp.float32)
    for piece, rows_of_group in zip(gathered, w_out_all):
        group_product = jnp.dot(
            piece, rows_of_group, preferred_element_type=jnp.float32
        )
        residual = residual + group_product.astype(jnp.bfloat16).astype(jnp.float32)
    normed_two = (
        residual * lax.rsqrt(jnp.mean(residual * residual, axis=1, keepdims=True) + EPS) * mlp_gain
    ).astype(jnp.bfloat16)
    gate_out = jnp.dot(normed_two, w_gate, preferred_element_type=jnp.float32)
    up_out = jnp.dot(normed_two, w_up, preferred_element_type=jnp.float32)
    hidden = (jax.nn.silu(gate_out) * up_out).astype(jnp.bfloat16)

    def unit_block(target):
        columns = lax.dynamic_slice_in_dim(w_down, target * quarter, quarter, 1)
        return jnp.dot(hidden, columns, preferred_element_type=jnp.float32).astype(jnp.bfloat16)

    arrived_parts = []
    for k in range(1, mlp_count):
        target = (part_index + k) % mlp_count
        arrived_parts.append(shift_mlp(unit_block(target), k, mlp_count))
    unit_share = unit_block(part_index).astype(jnp.float32)
    for part in arrived_parts:
        unit_share = unit_share + part.astype(jnp.float32)
    residual_share = lax.dynamic_slice_in_dim(residual, part_index * quarter, quarter, 1)
    result = (residual_share + unit_share).astype(jnp.bfloat16)
    return (result.reshape(per_owner_rows, tokens, quarter), accepted_rows)


def solution(mesh):
    placed = (
        P("req", None, "mlp"),
        P(),
        P("req"),
        P("req", None),
        P("req", None),
        P("req", None, "mlp", None),
        P(),
        P(None, "mlp"),
        P(None, "mlp"),
        P("mlp", None),
        P(),
        P(None, "mlp"),
        P(None, "mlp"),
        P("mlp", None),
    )
    return jax.shard_map(
        per_device,
        mesh=mesh,
        in_specs=placed,
        out_specs=(P("req", None, "mlp"), P("req", None, "mlp", None)),
        check_vma=False,
    )
```

```python
import functools
import math

import jax
import jax.numpy as jnp
from jax import lax
from jax.sharding import PartitionSpec as P

from jax.experimental import pallas as pl
from jax.experimental.pallas import tpu as pltpu


HEAD_DIM = 64


EPS = 1e-06
HIGH = lax.Precision.HIGHEST


def ancestry(tree_links, tokens):
    parent_link = (
        tree_links[:, :, None] == jnp.arange(tokens, dtype=jnp.int32)[None, None, :]
    ).astype(jnp.float32)
    reachable = jnp.maximum(parent_link, jnp.eye(tokens, dtype=jnp.float32)[None])
    for _ in range(max(tokens - 1, 1).bit_length()):
        reachable = jnp.minimum(
            jnp.einsum("rij,rjk->rik", reachable, reachable, precision=HIGH), 1.0
        )
    return reachable > 0.5


def shift_mlp(value, shift, count):
    return lax.ppermute(value, "mlp", [(i, (i + shift) % count) for i in range(count)])


def pieces_mlp(value, count):
    return [value] + [shift_mlp(value, k, count) for k in range(1, count)]


def place_blocks(pieces, count, part_index):
    width = pieces[0].shape[-1]
    full = jnp.zeros(pieces[0].shape[:-1] + (width * count,), pieces[0].dtype)
    for k, piece in enumerate(pieces):
        offset = ((part_index - k) % count) * width
        full = lax.dynamic_update_slice_in_dim(full, piece, offset, full.ndim - 1)
    return full


def attend_kernel(source_ref, length_ref, row_ref, cache_ref, mask_ref, out_ref, *, widths):
    for slot in range(cache_ref.shape[0]):
        attend_slot(source_ref, length_ref, row_ref, cache_ref, mask_ref, out_ref, slot, widths)


def attend_slot(source_ref, length_ref, row_ref, cache_ref, mask_ref, out_ref, slot, widths):
    query_width, group_heads = widths
    source = source_ref[slot]
    row = row_ref[source]
    tokens = row.shape[0]
    cache = cache_ref[slot]
    keys_cache = cache[:, :HEAD_DIM].T
    values_cache = cache[:, HEAD_DIM:]
    fresh = row[:, 2 * query_width :]
    keys_draft = fresh[:, :HEAD_DIM].T
    values_draft = fresh[:, HEAD_DIM:]
    live = lax.broadcasted_iota(jnp.int32, (1, cache.shape[0]), 1) < length_ref[slot]
    visible = jnp.concatenate([mask_ref[slot]] * group_heads, axis=0) > 0.5
    scale = 1.0 / math.sqrt(HEAD_DIM)

    def stacked(offset):
        return jnp.concatenate(
            [row[:, offset + g * HEAD_DIM : offset + (g + 1) * HEAD_DIM] for g in range(group_heads)],
            axis=0,
        )

    high, low = stacked(0), stacked(query_width)

    def times(keys):
        return (
            jnp.dot(high, keys, preferred_element_type=jnp.float32)
            + jnp.dot(low, keys, preferred_element_type=jnp.float32)
        ) * scale

    score_cache = jnp.where(live, times(keys_cache), -jnp.inf)
    score_draft = jnp.where(visible, times(keys_draft), -jnp.inf)
    top = jnp.maximum(
        jnp.max(score_cache, axis=1, keepdims=True), jnp.max(score_draft, axis=1, keepdims=True)
    )
    weight_cache = jnp.exp(score_cache - top).astype(jnp.bfloat16)
    weight_draft = jnp.exp(score_draft - top).astype(jnp.bfloat16)
    numerator = jnp.dot(weight_cache, values_cache, preferred_element_type=jnp.float32) + jnp.dot(
        weight_draft, values_draft, preferred_element_type=jnp.float32
    )
    denominator = jnp.sum(weight_cache.astype(jnp.float32), axis=1, keepdims=True) + jnp.sum(
        weight_draft.astype(jnp.float32), axis=1, keepdims=True
    )
    attended = (numerator / denominator).astype(jnp.bfloat16)
    out_ref[source] = jnp.concatenate(
        [attended[g * tokens : (g + 1) * tokens] for g in range(group_heads)], axis=1
    )


def per_device(
    drafts,
    slot_of,
    lengths,
    parents,
    accepted_tokens,
    cached_key_value,
    attn_gain,
    query_weight,
    key_value_weight,
    w_out,
    mlp_gain,
    w_gate,
    w_up,
    w_down,
):
    req_count = lax.axis_size("req")
    mlp_count = lax.axis_size("mlp")
    my_index = lax.axis_index("req")
    part_index = lax.axis_index("mlp")
    per_owner_rows, tokens, quarter = drafts.shape

    w_out_all = pieces_mlp(w_out, mlp_count)

    local_ids = jnp.arange(per_owner_rows, dtype=jnp.int32)
    devices = jnp.arange(req_count, dtype=jnp.int32)
    my_slots = lax.dynamic_slice_in_dim(slot_of, my_index * per_owner_rows, per_owner_rows)
    my_owners = my_slots // per_owner_rows
    send_pick = jnp.sum(
        jnp.where(my_owners[None, :] == devices[:, None], local_ids[None, :], 0), axis=1
    )
    owned_slots = my_index * per_owner_rows + local_ids
    requests = jnp.arange(slot_of.shape[0], dtype=jnp.int32)
    request_of = jnp.sum(
        jnp.where(slot_of[None, :] == owned_slots[:, None], requests[None, :], 0), axis=1
    )
    source_of = request_of // per_owner_rows

    rows = per_owner_rows * tokens
    owned_pieces = pieces_mlp(drafts.reshape(rows, quarter), mlp_count)
    owned_all = place_blocks(owned_pieces, mlp_count, part_index)
    wide_rows = owned_all.astype(jnp.float32)
    normalized_rows = (
        wide_rows
        * lax.rsqrt(jnp.mean(wide_rows * wide_rows, axis=1, keepdims=True) + EPS)
        * attn_gain
    ).astype(jnp.bfloat16)
    kv_heads = key_value_weight.shape[1] // (2 * HEAD_DIM)
    group_heads = query_weight.shape[1] // (kv_heads * HEAD_DIM)
    query_width = kv_heads * group_heads * HEAD_DIM
    queries = jnp.dot(normalized_rows, query_weight, preferred_element_type=jnp.float32)
    fresh = jnp.dot(normalized_rows, key_value_weight, preferred_element_type=jnp.float32).astype(
        jnp.bfloat16
    )
    query_high = queries.astype(jnp.bfloat16)
    query_low = (queries - query_high.astype(jnp.float32)).astype(jnp.bfloat16)
    payload = jnp.concatenate([query_high, query_low, fresh], axis=1).reshape(
        per_owner_rows, tokens, -1
    )

    outgoing = jnp.take(payload, send_pick, axis=0, mode="clip")
    incoming = lax.all_to_all(outgoing, "req", 0, 0, tiled=True)
    local_rows = jnp.take(incoming, source_of, axis=0, mode="clip")
    new_key_value = local_rows[..., 2 * query_width :].reshape(
        per_owner_rows, tokens, kv_heads, 2 * HEAD_DIM
    )
    picker = (
        accepted_tokens[:, :, None] == jnp.arange(tokens, dtype=jnp.int32)[None, None, :]
    ).astype(jnp.bfloat16)
    accepted_rows = jnp.einsum(
        "rat,rtkd->rakd", picker, new_key_value, preferred_element_type=jnp.float32
    ).astype(jnp.bfloat16)

    visible = ancestry(parents, tokens).astype(jnp.float32)
    head_width = kv_heads * group_heads * HEAD_DIM
    cache_len = cached_key_value.shape[1]
    grid_spec = pltpu.PrefetchScalarGridSpec(
        num_scalar_prefetch=2,
        grid=(1,),
        in_specs=[
            pl.BlockSpec(incoming.shape, lambda j, src, lens: (0, 0, 0)),
            pl.BlockSpec((per_owner_rows, cache_len, 2 * HEAD_DIM), lambda j, src, lens: (0, 0, 0)),
            pl.BlockSpec((per_owner_rows, tokens, tokens), lambda j, src, lens: (0, 0, 0)),
        ],
        out_specs=pl.BlockSpec((req_count, tokens, head_width), lambda j, src, lens: (0, 0, 0)),
    )
    returning = pl.pallas_call(
        functools.partial(attend_kernel, widths=(query_width, group_heads)),
        grid_spec=grid_spec,
        out_shape=jax.ShapeDtypeStruct((req_count, tokens, head_width), jnp.bfloat16),
    )(
        source_of,
        lengths,
        incoming,
        cached_key_value.reshape(per_owner_rows, cache_len, 2 * HEAD_DIM),
        visible,
    )

    arrived = lax.all_to_all(returning, "req", 0, 0, tiled=True)
    back_rows = jnp.take(arrived, my_owners, axis=0, mode="clip")

    gathered = pieces_mlp(back_rows.reshape(rows, head_width), mlp_count)

    residual = owned_all.astype(jnp.float32)
    for piece, rows_of_group in zip(gathered, w_out_all):
        group_product = jnp.dot(
            piece, rows_of_group, preferred_element_type=jnp.float32
        )
        residual = residual + group_product.astype(jnp.bfloat16).astype(jnp.float32)
    normed_two = (
        residual * lax.rsqrt(jnp.mean(residual * residual, axis=1, keepdims=True) + EPS) * mlp_gain
    ).astype(jnp.bfloat16)
    gate_out = jnp.dot(normed_two, w_gate, preferred_element_type=jnp.float32)
    up_out = jnp.dot(normed_two, w_up, preferred_element_type=jnp.float32)
    hidden = (jax.nn.silu(gate_out) * up_out).astype(jnp.bfloat16)

    def unit_block(target):
        columns = lax.dynamic_slice_in_dim(w_down, target * quarter, quarter, 1)
        return jnp.dot(hidden, columns, preferred_element_type=jnp.float32).astype(jnp.bfloat16)

    arrived_parts = []
    for k in range(1, mlp_count):
        target = (part_index + k) % mlp_count
        arrived_parts.append(shift_mlp(unit_block(target), k, mlp_count))
    unit_share = unit_block(part_index).astype(jnp.float32)
    for part in arrived_parts:
        unit_share = unit_share + part.astype(jnp.float32)
    residual_share = lax.dynamic_slice_in_dim(residual, part_index * quarter, quarter, 1)
    result = (residual_share + unit_share).astype(jnp.bfloat16)
    return (result.reshape(per_owner_rows, tokens, quarter), accepted_rows)


def solution(mesh):
    placed = (
        P("req", None, "mlp"),
        P(),
        P("req"),
        P("req", None),
        P("req", None),
        P("req", None, "mlp", None),
        P(),
        P(None, "mlp"),
        P(None, "mlp"),
        P("mlp", None),
        P(),
        P(None, "mlp"),
        P(None, "mlp"),
        P("mlp", None),
    )
    return jax.shard_map(
        per_device,
        mesh=mesh,
        in_specs=placed,
        out_specs=(P("req", None, "mlp"), P("req", None, "mlp", None)),
        check_vma=False,
    )
```

```python
import functools
import math

import jax
import jax.numpy as jnp
from jax import lax
from jax.sharding import PartitionSpec as P

from jax.experimental import pallas as pl
from jax.experimental.pallas import tpu as pltpu


HEAD_DIM = 64


EPS = 1e-06
HIGH = lax.Precision.HIGHEST


def ancestry(tree_links, tokens):
    parent_link = (
        tree_links[:, :, None] == jnp.arange(tokens, dtype=jnp.int32)[None, None, :]
    ).astype(jnp.float32)
    reachable = jnp.maximum(parent_link, jnp.eye(tokens, dtype=jnp.float32)[None])
    for _ in range(max(tokens - 1, 1).bit_length()):
        reachable = jnp.minimum(
            jnp.einsum("rij,rjk->rik", reachable, reachable, precision=HIGH), 1.0
        )
    return reachable > 0.5


def shift_mlp(value, shift, count):
    return lax.ppermute(value, "mlp", [(i, (i + shift) % count) for i in range(count)])


def pieces_mlp(value, count):
    return [value] + [shift_mlp(value, k, count) for k in range(1, count)]


def place_blocks(pieces, count, part_index):
    width = pieces[0].shape[-1]
    full = jnp.zeros(pieces[0].shape[:-1] + (width * count,), pieces[0].dtype)
    for k, piece in enumerate(pieces):
        offset = ((part_index - k) % count) * width
        full = lax.dynamic_update_slice_in_dim(full, piece, offset, full.ndim - 1)
    return full


def attend_kernel(source_ref, length_ref, row_ref, cache_ref, mask_ref, out_ref, *, widths):
    for slot in range(cache_ref.shape[0]):
        attend_slot(source_ref, length_ref, row_ref, cache_ref, mask_ref, out_ref, slot, widths)


def attend_slot(source_ref, length_ref, row_ref, cache_ref, mask_ref, out_ref, slot, widths):
    query_width, group_heads = widths
    source = source_ref[slot]
    row = row_ref[source]
    tokens = row.shape[0]
    cache = cache_ref[slot]
    keys_cache = cache[:, :HEAD_DIM].T
    values_cache = cache[:, HEAD_DIM:]
    fresh = row[:, 2 * query_width :]
    keys_draft = fresh[:, :HEAD_DIM].T
    values_draft = fresh[:, HEAD_DIM:]
    live = lax.broadcasted_iota(jnp.int32, (1, cache.shape[0]), 1) < length_ref[slot]
    visible = jnp.concatenate([mask_ref[slot]] * group_heads, axis=0) > 0.5
    scale = 1.0 / math.sqrt(HEAD_DIM)

    def stacked(offset):
        return jnp.concatenate(
            [row[:, offset + g * HEAD_DIM : offset + (g + 1) * HEAD_DIM] for g in range(group_heads)],
            axis=0,
        )

    parts = jnp.concatenate([stacked(0), stacked(query_width)], axis=0)
    rows = parts.shape[0] // 2

    def times(keys):
        both = jnp.dot(parts, keys, preferred_element_type=jnp.float32)
        return (both[:rows] + both[rows:]) * scale

    score_cache = jnp.where(live, times(keys_cache), -jnp.inf)
    score_draft = jnp.where(visible, times(keys_draft), -jnp.inf)
    top = jnp.maximum(
        jnp.max(score_cache, axis=1, keepdims=True), jnp.max(score_draft, axis=1, keepdims=True)
    )
    weight_cache = jnp.exp(score_cache - top).astype(jnp.bfloat16)
    weight_draft = jnp.exp(score_draft - top).astype(jnp.bfloat16)
    numerator = jnp.dot(weight_cache, values_cache, preferred_element_type=jnp.float32) + jnp.dot(
        weight_draft, values_draft, preferred_element_type=jnp.float32
    )
    denominator = jnp.sum(weight_cache.astype(jnp.float32), axis=1, keepdims=True) + jnp.sum(
        weight_draft.astype(jnp.float32), axis=1, keepdims=True
    )
    attended = (numerator / denominator).astype(jnp.bfloat16)
    out_ref[source] = jnp.concatenate(
        [attended[g * tokens : (g + 1) * tokens] for g in range(group_heads)], axis=1
    )


def per_device(
    drafts,
    slot_of,
    lengths,
    parents,
    accepted_tokens,
    cached_key_value,
    attn_gain,
    query_weight,
    key_value_weight,
    w_out,
    mlp_gain,
    w_gate,
    w_up,
    w_down,
):
    req_count = lax.axis_size("req")
    mlp_count = lax.axis_size("mlp")
    my_index = lax.axis_index("req")
    part_index = lax.axis_index("mlp")
    per_owner_rows, tokens, quarter = drafts.shape

    w_out_all = pieces_mlp(w_out, mlp_count)

    local_ids = jnp.arange(per_owner_rows, dtype=jnp.int32)
    devices = jnp.arange(req_count, dtype=jnp.int32)
    my_slots = lax.dynamic_slice_in_dim(slot_of, my_index * per_owner_rows, per_owner_rows)
    my_owners = my_slots // per_owner_rows
    send_pick = jnp.sum(
        jnp.where(my_owners[None, :] == devices[:, None], local_ids[None, :], 0), axis=1
    )
    owned_slots = my_index * per_owner_rows + local_ids
    requests = jnp.arange(slot_of.shape[0], dtype=jnp.int32)
    request_of = jnp.sum(
        jnp.where(slot_of[None, :] == owned_slots[:, None], requests[None, :], 0), axis=1
    )
    source_of = request_of // per_owner_rows

    rows = per_owner_rows * tokens
    owned_pieces = pieces_mlp(drafts.reshape(rows, quarter), mlp_count)
    owned_all = place_blocks(owned_pieces, mlp_count, part_index)
    wide_rows = owned_all.astype(jnp.float32)
    normalized_rows = (
        wide_rows
        * lax.rsqrt(jnp.mean(wide_rows * wide_rows, axis=1, keepdims=True) + EPS)
        * attn_gain
    ).astype(jnp.bfloat16)
    kv_heads = key_value_weight.shape[1] // (2 * HEAD_DIM)
    group_heads = query_weight.shape[1] // (kv_heads * HEAD_DIM)
    query_width = kv_heads * group_heads * HEAD_DIM
    queries = jnp.dot(normalized_rows, query_weight, preferred_element_type=jnp.float32)
    fresh = jnp.dot(normalized_rows, key_value_weight, preferred_element_type=jnp.float32).astype(
        jnp.bfloat16
    )
    query_high = queries.astype(jnp.bfloat16)
    query_low = (queries - query_high.astype(jnp.float32)).astype(jnp.bfloat16)
    payload = jnp.concatenate([query_high, query_low, fresh], axis=1).reshape(
        per_owner_rows, tokens, -1
    )

    outgoing = jnp.take(payload, send_pick, axis=0, mode="clip")
    incoming = lax.all_to_all(outgoing, "req", 0, 0, tiled=True)
    local_rows = jnp.take(incoming, source_of, axis=0, mode="clip")
    new_key_value = local_rows[..., 2 * query_width :].reshape(
        per_owner_rows, tokens, kv_heads, 2 * HEAD_DIM
    )
    picker = (
        accepted_tokens[:, :, None] == jnp.arange(tokens, dtype=jnp.int32)[None, None, :]
    ).astype(jnp.bfloat16)
    accepted_rows = jnp.einsum(
        "rat,rtkd->rakd", picker, new_key_value, preferred_element_type=jnp.float32
    ).astype(jnp.bfloat16)

    visible = ancestry(parents, tokens).astype(jnp.float32)
    head_width = kv_heads * group_heads * HEAD_DIM
    cache_len = cached_key_value.shape[1]
    grid_spec = pltpu.PrefetchScalarGridSpec(
        num_scalar_prefetch=2,
        grid=(1,),
        in_specs=[
            pl.BlockSpec(incoming.shape, lambda j, src, lens: (0, 0, 0)),
            pl.BlockSpec((per_owner_rows, cache_len, 2 * HEAD_DIM), lambda j, src, lens: (0, 0, 0)),
            pl.BlockSpec((per_owner_rows, tokens, tokens), lambda j, src, lens: (0, 0, 0)),
        ],
        out_specs=pl.BlockSpec((req_count, tokens, head_width), lambda j, src, lens: (0, 0, 0)),
    )
    returning = pl.pallas_call(
        functools.partial(attend_kernel, widths=(query_width, group_heads)),
        grid_spec=grid_spec,
        out_shape=jax.ShapeDtypeStruct((req_count, tokens, head_width), jnp.bfloat16),
    )(
        source_of,
        lengths,
        incoming,
        cached_key_value.reshape(per_owner_rows, cache_len, 2 * HEAD_DIM),
        visible,
    )

    arrived = lax.all_to_all(returning, "req", 0, 0, tiled=True)
    back_rows = jnp.take(arrived, my_owners, axis=0, mode="clip")

    gathered = pieces_mlp(back_rows.reshape(rows, head_width), mlp_count)

    residual = owned_all.astype(jnp.float32)
    for piece, rows_of_group in zip(gathered, w_out_all):
        group_product = jnp.dot(
            piece, rows_of_group, preferred_element_type=jnp.float32
        )
        residual = residual + group_product.astype(jnp.bfloat16).astype(jnp.float32)
    normed_two = (
        residual * lax.rsqrt(jnp.mean(residual * residual, axis=1, keepdims=True) + EPS) * mlp_gain
    ).astype(jnp.bfloat16)
    gate_out = jnp.dot(normed_two, w_gate, preferred_element_type=jnp.float32)
    up_out = jnp.dot(normed_two, w_up, preferred_element_type=jnp.float32)
    hidden = (jax.nn.silu(gate_out) * up_out).astype(jnp.bfloat16)

    def unit_block(target):
        columns = lax.dynamic_slice_in_dim(w_down, target * quarter, quarter, 1)
        return jnp.dot(hidden, columns, preferred_element_type=jnp.float32).astype(jnp.bfloat16)

    arrived_parts = []
    for k in range(1, mlp_count):
        target = (part_index + k) % mlp_count
        arrived_parts.append(shift_mlp(unit_block(target), k, mlp_count))
    unit_share = unit_block(part_index).astype(jnp.float32)
    for part in arrived_parts:
        unit_share = unit_share + part.astype(jnp.float32)
    residual_share = lax.dynamic_slice_in_dim(residual, part_index * quarter, quarter, 1)
    result = (residual_share + unit_share).astype(jnp.bfloat16)
    return (result.reshape(per_owner_rows, tokens, quarter), accepted_rows)


def solution(mesh):
    placed = (
        P("req", None, "mlp"),
        P(),
        P("req"),
        P("req", None),
        P("req", None),
        P("req", None, "mlp", None),
        P(),
        P(None, "mlp"),
        P(None, "mlp"),
        P("mlp", None),
        P(),
        P(None, "mlp"),
        P(None, "mlp"),
        P("mlp", None),
    )
    return jax.shard_map(
        per_device,
        mesh=mesh,
        in_specs=placed,
        out_specs=(P("req", None, "mlp"), P("req", None, "mlp", None)),
        check_vma=False,
    )
```
